32 devices in a mesh: cluster: 4 (over y, x), fsdp: 8 (over z, core).
Axes of the slice: x: 2, y: 2, z: 4, core: 2. Of those that a mesh axis runs over, the one named last changes fastest.
Arguments:
- gate_pre: bfloat16 [4, 2048, 4608], P('cluster', 'fsdp'), may hold values from -8 to 8
- up_pre: bfloat16 [4, 2048, 4608], P('cluster', 'fsdp'), may hold values from -6 to 6
- cotangent: bfloat16 [4, 2048, 2304], P('cluster', 'fsdp'), may hold values from -6 to 6
- down_weight: float32 [4, 4608, 2304], P('cluster', 'fsdp'), may hold values from -0.09375 to 0.09375
- first_moment: float32 [4, 4608, 2304], P('cluster', 'fsdp'), may hold values from -18 to 18
- second_moment: float32 [4, 4608, 2304], P('cluster', 'fsdp'), may hold values from 100 to 3000
- pseudo_grad: float32 [4, 512, 2304], P('cluster', 'fsdp'), may hold values from -6 to 6
- outer_params: float32 [512, 2304], P('fsdp'), may hold values from -6 to 6
- outer_momentum: float32 [512, 2304], P('fsdp'), may hold values from -3 to 3
Outputs:
- gate_grad: bfloat16 [4, 2048, 4608], P('cluster', 'fsdp')
- up_grad: bfloat16 [4, 2048, 4608], P('cluster', 'fsdp')
- new_weight: float32 [4, 4608, 2304], P('cluster', 'fsdp')
- new_first: float32 [4, 4608, 2304], P('cluster', 'fsdp')
- new_second: float32 [4, 4608, 2304], P('cluster', 'fsdp')
- new_outer: float32 [512, 2304], P('fsdp')
- new_momentum: float32 [512, 2304], P('fsdp')
The draws below stay inside these ranges and needn't reach their ends.
All inputs are finite; a program needn't handle non-finite values.
Results may differ from the reference program's by a relative error of at most 0.02.
Values may be sent and summed in bfloat16 or wider, within the bound.
No kernel may reach another device: no remote copies, remote signals or barrier semaphores. Data moves between devices by JAX's collectives and lax.ppermute only.
A program may use at most 192 MiB of HBM per device.

```python
import math
import jax
import jax.numpy as jnp
from jax import lax

D = 2304
FF = 4608
TOK_DEV = 256
FRAG_ROWS = 512
CLUSTER_TOK = 2048
N_CLUSTER = 4


def levels(own_key, extent, split, low, high):
    def one(dim, blocks):
        draws = jax.random.uniform(jax.random.fold_in(jax.random.fold_in(own_key, 6), dim), (blocks,), jnp.float32, low / len(split), high / len(split))
        return jnp.repeat(jnp.exp(draws), extent[dim] // blocks).reshape((-1,) + (1,) * (len(extent) - dim - 1))

    factor_of = one(*split[0])
    for cut in split[1:]:
        factor_of = factor_of * one(*cut)
    return factor_of


def scatter_about(rng, shape, deviation, reach, cuts=(), dtype=jnp.bfloat16):
    array = deviation * jax.random.normal(rng, shape, jnp.float32)
    if cuts:
        array = array * levels(rng, shape, cuts, -0.22, 0.18)
    return jnp.clip(array, -reach, reach).astype(dtype)


def setup_inputs(seed: int = 0) -> dict:
    seeds = jax.random.split(jax.random.key(seed), 10)
    gate_pre = scatter_about(seeds[0], (N_CLUSTER, CLUSTER_TOK, FF), 1.5, 8.0, ((0, 4), (1, 8)))
    up_pre = scatter_about(seeds[1], (N_CLUSTER, CLUSTER_TOK, FF), 1.0, 6.0, ((0, 4), (1, 8)))
    cotangent = scatter_about(seeds[2], (N_CLUSTER, CLUSTER_TOK, D), 1.0, 6.0, ((0, 4), (1, 8)))
    down_weight = scatter_about(seeds[3], (N_CLUSTER, FF, D), FF ** -0.5, 0.09375, ((0, 4), (1, 8)), jnp.float32)
    first_moment = scatter_about(seeds[4], (N_CLUSTER, FF, D), 3.0, 18.0, ((0, 4), (1, 8)), jnp.float32)
    second_moment = jnp.clip(jnp.exp(math.log(3000.0) - 3.4011974 * jax.random.uniform(seeds[5], (N_CLUSTER, FF, D), jnp.float32) ** levels(seeds[5], (N_CLUSTER, FF, D), ((0, 4), (1, 8)), -0.2, 0.2)), 100.0, 3000.0)
    pseudo_grad = scatter_about(seeds[6], (N_CLUSTER, FRAG_ROWS, D), 1.0, 6.0, ((0, 4), (1, 8)), jnp.float32)
    outer_params = scatter_about(seeds[7], (FRAG_ROWS, D), 1.0, 6.0, ((0, 8),), jnp.float32)
    outer_momentum = scatter_about(seeds[8], (FRAG_ROWS, D), 0.5, 3.0, ((0, 8),), jnp.float32)
    return dict(gate_pre=gate_pre, up_pre=up_pre, cotangent=cotangent, down_weight=down_weight, first_moment=first_moment, second_moment=second_moment, pseudo_grad=pseudo_grad, outer_params=outer_params, outer_momentum=outer_momentum)


def swish_parts(gate_pre, up_pre):
    gate_f = gate_pre.astype(jnp.float32)
    up_f = up_pre.astype(jnp.float32)
    sigma_gate = jax.nn.sigmoid(gate_f)
    active = gate_f * sigma_gate
    hidden = (active * up_f).astype(jnp.bfloat16)
    return (gate_f, up_f, sigma_gate, active, hidden)

def cluster_step(gate_pre, up_pre, cotangent, weight, first, second):
    gate_f, up_f, sigma_gate, active, hidden = swish_parts(gate_pre, up_pre)
    weight_bf = weight.astype(jnp.bfloat16)
    dhid = lax.dot_general(cotangent, weight_bf, (((1,), (1,)), ((), ())), preferred_element_type=jnp.float32)
    gate_grad = (dhid * up_f * sigma_gate * (1.0 + gate_f * (1.0 - sigma_gate))).astype(jnp.bfloat16)
    up_grad = (dhid * active).astype(jnp.bfloat16)
    blocks = hidden.shape[0] // TOK_DEV
    hidden_blocks = hidden.reshape(blocks, TOK_DEV, FF)
    cot_blocks = cotangent.reshape(blocks, TOK_DEV, D)

    def add_block(running, paired):
        hidden_rows, cot_rows = paired
        part = jnp.dot(hidden_rows.T, cot_rows, preferred_element_type=jnp.float32).astype(jnp.bfloat16)
        part = lax.optimization_barrier(part)
        return (running + part.astype(jnp.float32), None)
    grad, _ = lax.scan(add_block, jnp.zeros((FF, D), jnp.float32), (hidden_blocks, cot_blocks))
    new_first = 0.9 * first + 0.1 * grad
    new_second = 0.95 * second + 0.05 * grad * grad
    update = new_first / 0.6513215599 / (jnp.sqrt(new_second / 0.4012630607) + 1e-08) + 0.1 * weight
    new_weight = weight - 0.001 * update
    return (gate_grad, up_grad, new_weight, new_first, new_second)

def reference(gate_pre, up_pre, cotangent, down_weight, first_moment, second_moment, pseudo_grad, outer_params, outer_momentum):
    results = [cluster_step(gate_pre[c], up_pre[c], cotangent[c], down_weight[c], first_moment[c], second_moment[c]) for c in range(N_CLUSTER)]
    gate_grad = jnp.stack([r[0] for r in results])
    up_grad = jnp.stack([r[1] for r in results])
    new_weight = jnp.stack([r[2] for r in results])
    new_first = jnp.stack([r[3] for r in results])
    new_second = jnp.stack([r[4] for r in results])
    mean_delta = lax.optimization_barrier(jnp.sum(pseudo_grad, axis=0)) / N_CLUSTER
    new_momentum = 0.9 * outer_momentum + mean_delta
    new_outer = outer_params - 0.7 * (mean_delta + 0.9 * new_momentum)
    return (gate_grad, up_grad, new_weight, new_first, new_second, new_outer, new_momentum)
```

```python
import jax
import jax.numpy as jnp
from jax import lax
from jax.sharding import PartitionSpec as P

BLOCK_TOK = 256


def swish_parts(gate_pre, up_pre):
    gate_f = gate_pre.astype(jnp.float32)
    up_f = up_pre.astype(jnp.float32)
    sigma_gate = jax.nn.sigmoid(gate_f)
    active = gate_f * sigma_gate
    hidden = (active * up_f).astype(jnp.bfloat16)
    return (gate_f, up_f, sigma_gate, active, hidden)


def swish_grads(dhid, gate_f, up_f, sigma_gate, active):
    gate_grad = (dhid * up_f * sigma_gate * (1.0 + gate_f * (1.0 - sigma_gate))).astype(
        jnp.bfloat16
    )
    up_grad = (dhid * active).astype(jnp.bfloat16)
    return (gate_grad, up_grad)


def shards(
    gate_pre,
    up_pre,
    cotangent,
    down_weight,
    first_moment,
    second_moment,
    pseudo_grad,
    outer_params,
    outer_momentum,
):
    n = lax.axis_size("fsdp")
    gate_local = gate_pre[0]
    up_local = up_pre[0]
    cot_local = cotangent[0]
    weight = down_weight[0]
    tok, ff = gate_local.shape
    rows = weight.shape[0]
    weight_bf = weight.astype(jnp.bfloat16)

    cot_all = lax.all_gather(cot_local, "fsdp", axis=0, tiled=True)
    gate_f, up_f, sigma_gate, active, hidden = swish_parts(gate_local, up_local)
    hid_send = hidden.reshape(tok, n, rows).transpose(1, 0, 2)
    hid_cols = lax.all_to_all(hid_send, "fsdp", 0, 0, tiled=True)

    dhid_cols = lax.dot_general(
        cot_all, weight_bf, (((1,), (1,)), ((), ())), preferred_element_type=jnp.float32
    )
    dhid_recv = lax.all_to_all(dhid_cols.reshape(n, tok, rows), "fsdp", 0, 0, tiled=True)
    dhid = dhid_recv.transpose(1, 0, 2).reshape(tok, ff)
    gate_grad, up_grad = swish_grads(dhid, gate_f, up_f, sigma_gate, active)

    blocks = (n * tok) // BLOCK_TOK
    hid_blocks = hid_cols.reshape(blocks, BLOCK_TOK, rows)
    cot_blocks = cot_all.reshape(blocks, BLOCK_TOK, cot_all.shape[1])
    grad = None
    for k in range(blocks):
        part = lax.dot_general(
            hid_blocks[k], cot_blocks[k], (((0,), (0,)), ((), ())),
            preferred_element_type=jnp.float32,
        ).astype(jnp.bfloat16).astype(jnp.float32)
        grad = part if grad is None else grad + part

    new_first = 0.9 * first_moment[0] + 0.1 * grad
    new_second = 0.95 * second_moment[0] + 0.05 * grad * grad
    update = new_first / 0.6513215599 / (jnp.sqrt(new_second / 0.4012630607) + 1e-08) + 0.1 * weight
    new_weight = weight - 0.001 * update
    clusters = lax.axis_size("cluster")
    total = lax.psum(pseudo_grad[0].astype(jnp.bfloat16), "cluster").astype(jnp.float32)
    mean_delta = total / clusters
    new_momentum = 0.9 * outer_momentum + mean_delta
    new_outer = outer_params - 0.7 * (mean_delta + 0.9 * new_momentum)
    return (
        gate_grad[None],
        up_grad[None],
        new_weight[None],
        new_first[None],
        new_second[None],
        new_outer,
        new_momentum,
    )


def solution(mesh):
    in_specs = (
        P("cluster", "fsdp", None),
        P("cluster", "fsdp", None),
        P("cluster", "fsdp", None),
        P("cluster", "fsdp", None),
        P("cluster", "fsdp", None),
        P("cluster", "fsdp", None),
        P("cluster", "fsdp", None),
        P("fsdp", None),
        P("fsdp", None),
    )
    out_specs = (
        P("cluster", "fsdp", None),
        P("cluster", "fsdp", None),
        P("cluster", "fsdp", None),
        P("cluster", "fsdp", None),
        P("cluster", "fsdp", None),
        P("fsdp", None),
        P("fsdp", None),
    )
    return jax.shard_map(shards, mesh=mesh, in_specs=in_specs, out_specs=out_specs, check_vma=False)
```

```python
import jax
import jax.numpy as jnp
from jax import lax
from jax.sharding import PartitionSpec as P

BLOCK_TOK = 256


def swish_parts(gate_pre, up_pre):
    gate_f = gate_pre.astype(jnp.float32)
    up_f = up_pre.astype(jnp.float32)
    sigma_gate = jax.nn.sigmoid(gate_f)
    active = gate_f * sigma_gate
    hidden = (active * up_f).astype(jnp.bfloat16)
    return (gate_f, up_f, sigma_gate, active, hidden)


def swish_grads(dhid, gate_f, up_f, sigma_gate, active):
    gate_grad = (dhid * up_f * sigma_gate * (1.0 + gate_f * (1.0 - sigma_gate))).astype(
        jnp.bfloat16
    )
    up_grad = (dhid * active).astype(jnp.bfloat16)
    return (gate_grad, up_grad)


def shards(
    gate_pre,
    up_pre,
    cotangent,
    down_weight,
    first_moment,
    second_moment,
    pseudo_grad,
    outer_params,
    outer_momentum,
):
    n = lax.axis_size("fsdp")
    clusters = lax.axis_size("cluster")
    gate_local = gate_pre[0]
    up_local = up_pre[0]
    cot_local = cotangent[0]
    weight = down_weight[0]
    tok, ff = gate_local.shape
    rows = weight.shape[0]
    weight_bf = weight.astype(jnp.bfloat16)

    cot_all = lax.all_to_all(
        jnp.broadcast_to(cot_local[None], (n,) + cot_local.shape), "fsdp", 0, 0, tiled=True
    ).reshape(n * tok, cot_local.shape[1])
    gate_f, up_f, sigma_gate, active, hidden = swish_parts(gate_local, up_local)
    hid_send = hidden.reshape(tok, n, rows).transpose(1, 0, 2)
    hid_cols = lax.all_to_all(hid_send, "fsdp", 0, 0, tiled=True)

    dhid_cols = lax.dot_general(
        cot_all, weight_bf, (((1,), (1,)), ((), ())), preferred_element_type=jnp.float32
    )
    dhid_recv = lax.all_to_all(dhid_cols.reshape(n, tok, rows), "fsdp", 0, 0, tiled=True)
    dhid = dhid_recv.transpose(1, 0, 2).reshape(tok, ff)
    gate_grad, up_grad = swish_grads(dhid, gate_f, up_f, sigma_gate, active)

    blocks = (n * tok) // BLOCK_TOK
    hid_blocks = hid_cols.reshape(blocks, BLOCK_TOK, rows)
    cot_blocks = cot_all.reshape(blocks, BLOCK_TOK, cot_all.shape[1])
    grad = None
    for k in range(blocks):
        part = lax.dot_general(
            hid_blocks[k], cot_blocks[k], (((0,), (0,)), ((), ())),
            preferred_element_type=jnp.float32,
        ).astype(jnp.bfloat16).astype(jnp.float32)
        grad = part if grad is None else grad + part

    new_first = 0.9 * first_moment[0] + 0.1 * grad
    new_second = 0.95 * second_moment[0] + 0.05 * grad * grad
    update = new_first / 0.6513215599 / (jnp.sqrt(new_second / 0.4012630607) + 1e-08) + 0.1 * weight
    new_weight = weight - 0.001 * update
    delta_bf = pseudo_grad[0].astype(jnp.bfloat16)
    deltas = lax.all_to_all(
        jnp.broadcast_to(delta_bf[None], (clusters,) + delta_bf.shape), "cluster", 0, 0, tiled=True
    )
    total = jnp.sum(deltas.astype(jnp.float32), axis=0)
    mean_delta = total / clusters
    new_momentum = 0.9 * outer_momentum + mean_delta
    new_outer = outer_params - 0.7 * (mean_delta + 0.9 * new_momentum)
    return (
        gate_grad[None],
        up_grad[None],
        new_weight[None],
        new_first[None],
        new_second[None],
        new_outer,
        new_momentum,
    )


def solution(mesh):
    in_specs = (
        P("cluster", "fsdp", None),
        P("cluster", "fsdp", None),
        P("cluster", "fsdp", None),
        P("cluster", "fsdp", None),
        P("cluster", "fsdp", None),
        P("cluster", "fsdp", None),
        P("cluster", "fsdp", None),
        P("fsdp", None),
        P("fsdp", None),
    )
    out_specs = (
        P("cluster", "fsdp", None),
        P("cluster", "fsdp", None),
        P("cluster", "fsdp", None),
        P("cluster", "fsdp", None),
        P("cluster", "fsdp", None),
        P("fsdp", None),
        P("fsdp", None),
    )
    return jax.shard_map(shards, mesh=mesh, in_specs=in_specs, out_specs=out_specs, check_vma=False)
```

```python
import jax
import jax.numpy as jnp
from jax import lax
from jax.sharding import PartitionSpec as P

BLOCK_TOK = 256


def swish_parts(gate_pre, up_pre):
    gate_f = gate_pre.astype(jnp.float32)
    up_f = up_pre.astype(jnp.float32)
    sigma_gate = jax.nn.sigmoid(gate_f)
    active = gate_f * sigma_gate
    hidden = (active * up_f).astype(jnp.bfloat16)
    return (gate_f, up_f, sigma_gate, active, hidden)


def swish_grads(dhid, gate_f, up_f, sigma_gate, active):
    gate_grad = (dhid * up_f * sigma_gate * (1.0 + gate_f * (1.0 - sigma_gate))).astype(
        jnp.bfloat16
    )
    up_grad = (dhid * active).astype(jnp.bfloat16)
    return (gate_grad, up_grad)


def cluster_sum(delta_bf, clusters):
    held = delta_bf[None]
    if clusters & (clusters - 1) == 0:
        step = 1
        while step < clusters:
            perm = [(i, i ^ step) for i in range(clusters)]
            held = jnp.concatenate([held, lax.ppermute(held, "cluster", perm)], axis=0)
            step *= 2
    else:
        parts = [held]
        for s in range(1, clusters):
            perm = [(i, (i + s) % clusters) for i in range(clusters)]
            parts.append(lax.ppermute(held, "cluster", perm))
        held = jnp.concatenate(parts, axis=0)
    return jnp.sum(held.astype(jnp.float32), axis=0)


def shards(
    gate_pre,
    up_pre,
    cotangent,
    down_weight,
    first_moment,
    second_moment,
    pseudo_grad,
    outer_params,
    outer_momentum,
):
    n = lax.axis_size("fsdp")
    gate_local = gate_pre[0]
    up_local = up_pre[0]
    cot_local = cotangent[0]
    weight = down_weight[0]
    tok, ff = gate_local.shape
    rows = weight.shape[0]
    weight_bf = weight.astype(jnp.bfloat16)

    cot_all = lax.all_gather(cot_local, "fsdp", axis=0, tiled=True)
    gate_f, up_f, sigma_gate, active, hidden = swish_parts(gate_local, up_local)
    hid_send = hidden.reshape(tok, n, rows).transpose(1, 0, 2)
    hid_cols = lax.all_to_all(hid_send, "fsdp", 0, 0, tiled=True)

    dhid_cols = lax.dot_general(
        cot_all, weight_bf, (((1,), (1,)), ((), ())), preferred_element_type=jnp.float32
    )
    dhid_send = dhid_cols.astype(jnp.bfloat16).reshape(n, tok, rows)
    dhid_recv = lax.all_to_all(dhid_send, "fsdp", 0, 0, tiled=True)
    dhid = dhid_recv.transpose(1, 0, 2).reshape(tok, ff).astype(jnp.float32)
    gate_grad, up_grad = swish_grads(dhid, gate_f, up_f, sigma_gate, active)

    blocks = (n * tok) // BLOCK_TOK
    hid_blocks = hid_cols.reshape(blocks, BLOCK_TOK, rows)
    cot_blocks = cot_all.reshape(blocks, BLOCK_TOK, cot_all.shape[1])
    grad = None
    for k in range(blocks):
        part = lax.dot_general(
            hid_blocks[k], cot_blocks[k], (((0,), (0,)), ((), ())),
            preferred_element_type=jnp.float32,
        ).astype(jnp.bfloat16).astype(jnp.float32)
        grad = part if grad is None else grad + part

    new_first = 0.9 * first_moment[0] + 0.1 * grad
    new_second = 0.95 * second_moment[0] + 0.05 * grad * grad
    update = new_first / 0.6513215599 / (jnp.sqrt(new_second / 0.4012630607) + 1e-08) + 0.1 * weight
    new_weight = weight - 0.001 * update
    clusters = lax.axis_size("cluster")
    total = cluster_sum(pseudo_grad[0].astype(jnp.bfloat16), clusters)
    mean_delta = total / clusters
    new_momentum = 0.9 * outer_momentum + mean_delta
    new_outer = outer_params - 0.7 * (mean_delta + 0.9 * new_momentum)
    return (
        gate_grad[None],
        up_grad[None],
        new_weight[None],
        new_first[None],
        new_second[None],
        new_outer,
        new_momentum,
    )


def solution(mesh):
    in_specs = (
        P("cluster", "fsdp", None),
        P("cluster", "fsdp", None),
        P("cluster", "fsdp", None),
        P("cluster", "fsdp", None),
        P("cluster", "fsdp", None),
        P("cluster", "fsdp", None),
        P("cluster", "fsdp", None),
        P("fsdp", None),
        P("fsdp", None),
    )
    out_specs = (
        P("cluster", "fsdp", None),
        P("cluster", "fsdp", None),
        P("cluster", "fsdp", None),
        P("cluster", "fsdp", None),
        P("cluster", "fsdp", None),
        P("fsdp", None),
        P("fsdp", None),
    )
    return jax.shard_map(shards, mesh=mesh, in_specs=in_specs, out_specs=out_specs, check_vma=False)
```

```python
import jax
import jax.numpy as jnp
from jax import lax
from jax.sharding import PartitionSpec as P

BLOCK_TOK = 256


def swish_parts(gate_pre, up_pre):
    gate_f = gate_pre.astype(jnp.float32)
    up_f = up_pre.astype(jnp.float32)
    sigma_gate = jax.nn.sigmoid(gate_f)
    active = gate_f * sigma_gate
    hidden = (active * up_f).astype(jnp.bfloat16)
    return (gate_f, up_f, sigma_gate, active, hidden)


def swish_grads(dhid, gate_f, up_f, sigma_gate, active):
    gate_grad = (dhid * up_f * sigma_gate * (1.0 + gate_f * (1.0 - sigma_gate))).astype(
        jnp.bfloat16
    )
    up_grad = (dhid * active).astype(jnp.bfloat16)
    return (gate_grad, up_grad)


def cluster_sum(delta_bf, clusters):
    held = delta_bf[None]
    if clusters & (clusters - 1) == 0:
        step = 1
        while step < clusters:
            perm = [(i, i ^ step) for i in range(clusters)]
            held = jnp.concatenate([held, lax.ppermute(held, "cluster", perm)], axis=0)
            step *= 2
    else:
        parts = [held]
        for s in range(1, clusters):
            perm = [(i, (i + s) % clusters) for i in range(clusters)]
            parts.append(lax.ppermute(held, "cluster", perm))
        held = jnp.concatenate(parts, axis=0)
    return jnp.sum(held.astype(jnp.float32), axis=0)


def line_gather(x, n):
    m = n // 2
    f = lax.axis_index("fsdp")
    z = f // 2
    c = f % 2
    partner = [(i, i ^ 1) for i in range(n)]
    buf = jnp.zeros((n + 1,) + x.shape, x.dtype)

    def put(buf, blk, idx, valid):
        return lax.dynamic_update_slice(buf, blk[None], (jnp.where(valid, idx, n), 0, 0))

    buf = put(buf, x, f, True)
    buf = put(buf, lax.ppermute(x, "fsdp", partner), f ^ 1, True)
    right = x
    left = x
    for t in range(1, m):
        right = lax.ppermute(
            right, "fsdp", [(2 * q + k, 2 * (q + 1) + k) for q in range(t - 1, m - 1) for k in (0, 1)]
        )
        left = lax.ppermute(
            left, "fsdp", [(2 * q + k, 2 * (q - 1) + k) for q in range(1, m - t + 1) for k in (0, 1)]
        )
        ok_r = z >= t
        ok_l = z + t <= m - 1
        buf = put(buf, right, 2 * (z - t) + c, ok_r)
        buf = put(buf, left, 2 * (z + t) + c, ok_l)
        buf = put(buf, lax.ppermute(right, "fsdp", partner), 2 * (z - t) + 1 - c, ok_r)
        buf = put(buf, lax.ppermute(left, "fsdp", partner), 2 * (z + t) + 1 - c, ok_l)
    return buf


def shards(
    gate_pre,
    up_pre,
    cotangent,
    down_weight,
    first_moment,
    second_moment,
    pseudo_grad,
    outer_params,
    outer_momentum,
):
    n = lax.axis_size("fsdp")
    gate_local = gate_pre[0]
    up_local = up_pre[0]
    cot_local = cotangent[0]
    weight = down_weight[0]
    tok, ff = gate_local.shape
    rows = weight.shape[0]
    weight_bf = weight.astype(jnp.bfloat16)

    cot_all = line_gather(cot_local, n)[:n].reshape(n * tok, cot_local.shape[1])
    gate_f, up_f, sigma_gate, active, hidden = swish_parts(gate_local, up_local)
    hid_send = hidden.reshape(tok, n, rows).transpose(1, 0, 2)
    hid_cols = lax.all_to_all(hid_send, "fsdp", 0, 0, tiled=True)

    dhid_cols = lax.dot_general(
        cot_all, weight_bf, (((1,), (1,)), ((), ())), preferred_element_type=jnp.float32
    )
    dhid_send = dhid_cols.astype(jnp.bfloat16).reshape(n, tok, rows)
    dhid_recv = lax.all_to_all(dhid_send, "fsdp", 0, 0, tiled=True)
    dhid = dhid_recv.transpose(1, 0, 2).reshape(tok, ff).astype(jnp.float32)
    gate_grad, up_grad = swish_grads(dhid, gate_f, up_f, sigma_gate, active)

    blocks = (n * tok) // BLOCK_TOK
    hid_blocks = hid_cols.reshape(blocks, BLOCK_TOK, rows)
    cot_blocks = cot_all.reshape(blocks, BLOCK_TOK, cot_all.shape[1])
    grad = None
    for k in range(blocks):
        part = lax.dot_general(
            hid_blocks[k], cot_blocks[k], (((0,), (0,)), ((), ())),
            preferred_element_type=jnp.float32,
        ).astype(jnp.bfloat16).astype(jnp.float32)
        grad = part if grad is None else grad + part

    new_first = 0.9 * first_moment[0] + 0.1 * grad
    new_second = 0.95 * second_moment[0] + 0.05 * grad * grad
    update = new_first / 0.6513215599 / (jnp.sqrt(new_second / 0.4012630607) + 1e-08) + 0.1 * weight
    new_weight = weight - 0.001 * update
    clusters = lax.axis_size("cluster")
    total = cluster_sum(pseudo_grad[0].astype(jnp.bfloat16), clusters)
    mean_delta = total / clusters
    new_momentum = 0.9 * outer_momentum + mean_delta
    new_outer = outer_params - 0.7 * (mean_delta + 0.9 * new_momentum)
    return (
        gate_grad[None],
        up_grad[None],
        new_weight[None],
        new_first[None],
        new_second[None],
        new_outer,
        new_momentum,
    )


def solution(mesh):
    in_specs = (
        P("cluster", "fsdp", None),
        P("cluster", "fsdp", None),
        P("cluster", "fsdp", None),
        P("cluster", "fsdp", None),
        P("cluster", "fsdp", None),
        P("cluster", "fsdp", None),
        P("cluster", "fsdp", None),
        P("fsdp", None),
        P("fsdp", None),
    )
    out_specs = (
        P("cluster", "fsdp", None),
        P("cluster", "fsdp", None),
        P("cluster", "fsdp", None),
        P("cluster", "fsdp", None),
        P("cluster", "fsdp", None),
        P("fsdp", None),
        P("fsdp", None),
    )
    return jax.shard_map(shards, mesh=mesh, in_specs=in_specs, out_specs=out_specs, check_vma=False)
```

```python
import jax
import jax.numpy as jnp
from jax import lax
from jax.sharding import PartitionSpec as P

BLOCK_TOK = 256


def swish_parts(gate_pre, up_pre):
    gate_f = gate_pre.astype(jnp.float32)
    up_f = up_pre.astype(jnp.float32)
    sigma_gate = jax.nn.sigmoid(gate_f)
    active = gate_f * sigma_gate
    hidden = (active * up_f).astype(jnp.bfloat16)
    return (gate_f, up_f, sigma_gate, active, hidden)


def swish_grads(dhid, gate_f, up_f, sigma_gate, active):
    gate_grad = (dhid * up_f * sigma_gate * (1.0 + gate_f * (1.0 - sigma_gate))).astype(
        jnp.bfloat16
    )
    up_grad = (dhid * active).astype(jnp.bfloat16)
    return (gate_grad, up_grad)


def cluster_sum(delta_bf, clusters):
    held = delta_bf[None]
    if clusters & (clusters - 1) == 0:
        step = 1
        while step < clusters:
            perm = [(i, i ^ step) for i in range(clusters)]
            held = jnp.concatenate([held, lax.ppermute(held, "cluster", perm)], axis=0)
            step *= 2
    else:
        parts = [held]
        for s in range(1, clusters):
            perm = [(i, (i + s) % clusters) for i in range(clusters)]
            parts.append(lax.ppermute(held, "cluster", perm))
        held = jnp.concatenate(parts, axis=0)
    return jnp.sum(held.astype(jnp.float32), axis=0)


def shards(
    gate_pre,
    up_pre,
    cotangent,
    down_weight,
    first_moment,
    second_moment,
    pseudo_grad,
    outer_params,
    outer_momentum,
):
    n = lax.axis_size("fsdp")
    m = n // 2
    f = lax.axis_index("fsdp")
    z = f // 2
    c = f % 2
    gate_local = gate_pre[0]
    up_local = up_pre[0]
    cot_local = cotangent[0]
    weight = down_weight[0]
    tok, ff = gate_local.shape
    rows = weight.shape[0]
    weight_bf = weight.astype(jnp.bfloat16)
    per = tok // BLOCK_TOK

    gate_f, up_f, sigma_gate, active, hidden = swish_parts(gate_local, up_local)
    hid_send = hidden.reshape(tok, n, rows).transpose(1, 0, 2)
    hid_cols = lax.all_to_all(hid_send, "fsdp", 0, 0, tiled=True)

    def dhid_of(blk):
        return lax.dot_general(
            blk, weight_bf, (((1,), (1,)), ((), ())), preferred_element_type=jnp.float32
        ).astype(jnp.bfloat16)

    def grad_of(blk, src):
        hid = lax.dynamic_index_in_dim(hid_cols, src, 0, keepdims=False)
        total = None
        for b in range(per):
            rs = slice(b * BLOCK_TOK, (b + 1) * BLOCK_TOK)
            part = lax.dot_general(
                hid[rs], blk[rs], (((0,), (0,)), ((), ())), preferred_element_type=jnp.float32
            ).astype(jnp.bfloat16).astype(jnp.float32)
            total = part if total is None else total + part
        return total

    dbuf = jnp.zeros((n, tok, rows), jnp.bfloat16)

    def put(buf, blk, idx, valid):
        return lax.dynamic_update_slice(buf, blk[None], (jnp.where(valid, idx, f), 0, 0))

    partner = [(i, i ^ 1) for i in range(n)]
    grad = grad_of(cot_local, f)
    blk = lax.ppermute(cot_local, "fsdp", partner)
    dbuf = put(dbuf, lax.ppermute(dhid_of(blk), "fsdp", partner), f ^ 1, True)
    grad = grad + grad_of(blk, f ^ 1)
    right = cot_local
    left = cot_local
    for t in range(1, m):
        right = lax.ppermute(
            right, "fsdp", [(2 * q + k, 2 * (q + 1) + k) for q in range(t - 1, m - 1) for k in (0, 1)]
        )
        left = lax.ppermute(
            left, "fsdp", [(2 * q + k, 2 * (q - 1) + k) for q in range(1, m - t + 1) for k in (0, 1)]
        )
        p_right = lax.ppermute(right, "fsdp", partner)
        p_left = lax.ppermute(left, "fsdp", partner)
        ok_r = z >= t
        ok_l = z + t <= m - 1
        back_r = [(2 * q + k, 2 * (q - t) + k) for q in range(t, m) for k in (0, 1)]
        back_l = [(2 * q + k, 2 * (q + t) + k) for q in range(0, m - t) for k in (0, 1)]
        back_pr = [(2 * q + k, 2 * (q - t) + 1 - k) for q in range(t, m) for k in (0, 1)]
        back_pl = [(2 * q + k, 2 * (q + t) + 1 - k) for q in range(0, m - t) for k in (0, 1)]
        arrivals = (
            (right, 2 * (z - t) + c, ok_r, back_r, 2 * (z + t) + c, ok_l),
            (left, 2 * (z + t) + c, ok_l, back_l, 2 * (z - t) + c, ok_r),
            (p_right, 2 * (z - t) + 1 - c, ok_r, back_pr, 2 * (z + t) + 1 - c, ok_l),
            (p_left, 2 * (z + t) + 1 - c, ok_l, back_pl, 2 * (z - t) + 1 - c, ok_r),
        )
        for blk, src, ok, back, got, ok_got in arrivals:
            dbuf = put(dbuf, lax.ppermute(dhid_of(blk), "fsdp", back), got, ok_got)
            grad = grad + grad_of(blk, jnp.where(ok, src, f))
    dbuf = put(dbuf, dhid_of(cot_local), f, True)
    dhid = dbuf.transpose(1, 0, 2).reshape(tok, ff).astype(jnp.float32)
    gate_grad, up_grad = swish_grads(dhid, gate_f, up_f, sigma_gate, active)

    new_first = 0.9 * first_moment[0] + 0.1 * grad
    new_second = 0.95 * second_moment[0] + 0.05 * grad * grad
    update = new_first / 0.6513215599 / (jnp.sqrt(new_second / 0.4012630607) + 1e-08) + 0.1 * weight
    new_weight = weight - 0.001 * update
    clusters = lax.axis_size("cluster")
    total = cluster_sum(pseudo_grad[0].astype(jnp.bfloat16), clusters)
    mean_delta = total / clusters
    new_momentum = 0.9 * outer_momentum + mean_delta
    new_outer = outer_params - 0.7 * (mean_delta + 0.9 * new_momentum)
    return (
        gate_grad[None],
        up_grad[None],
        new_weight[None],
        new_first[None],
        new_second[None],
        new_outer,
        new_momentum,
    )


def solution(mesh):
    in_specs = (
        P("cluster", "fsdp", None),
        P("cluster", "fsdp", None),
        P("cluster", "fsdp", None),
        P("cluster", "fsdp", None),
        P("cluster", "fsdp", None),
        P("cluster", "fsdp", None),
        P("cluster", "fsdp", None),
        P("fsdp", None),
        P("fsdp", None),
    )
    out_specs = (
        P("cluster", "fsdp", None),
        P("cluster", "fsdp", None),
        P("cluster", "fsdp", None),
        P("cluster", "fsdp", None),
        P("cluster", "fsdp", None),
        P("fsdp", None),
        P("fsdp", None),
    )
    return jax.shard_map(shards, mesh=mesh, in_specs=in_specs, out_specs=out_specs, check_vma=False)
```

```python
import jax
import jax.numpy as jnp
from jax import lax
from jax.sharding import PartitionSpec as P

BLOCK_TOK = 256


def swish_parts(gate_pre, up_pre):
    gate_f = gate_pre.astype(jnp.float32)
    up_f = up_pre.astype(jnp.float32)
    sigma_gate = jax.nn.sigmoid(gate_f)
    active = gate_f * sigma_gate
    hidden = (active * up_f).astype(jnp.bfloat16)
    return (gate_f, up_f, sigma_gate, active, hidden)


def swish_grads(dhid, gate_f, up_f, sigma_gate, active):
    gate_grad = (dhid * up_f * sigma_gate * (1.0 + gate_f * (1.0 - sigma_gate))).astype(
        jnp.bfloat16
    )
    up_grad = (dhid * active).astype(jnp.bfloat16)
    return (gate_grad, up_grad)


def cluster_sum(delta_bf, clusters):
    held = delta_bf[None]
    if clusters & (clusters - 1) == 0:
        step = 1
        while step < clusters:
            perm = [(i, i ^ step) for i in range(clusters)]
            held = jnp.concatenate([held, lax.ppermute(held, "cluster", perm)], axis=0)
            step *= 2
    else:
        parts = [held]
        for s in range(1, clusters):
            perm = [(i, (i + s) % clusters) for i in range(clusters)]
            parts.append(lax.ppermute(held, "cluster", perm))
        held = jnp.concatenate(parts, axis=0)
    return jnp.sum(held.astype(jnp.float32), axis=0)


def shards(
    gate_pre,
    up_pre,
    cotangent,
    down_weight,
    first_moment,
    second_moment,
    pseudo_grad,
    outer_params,
    outer_momentum,
):
    n = lax.axis_size("fsdp")
    m = n // 2
    f = lax.axis_index("fsdp")
    z = f // 2
    c = f % 2
    gate_local = gate_pre[0]
    up_local = up_pre[0]
    cot_local = cotangent[0]
    weight = down_weight[0]
    tok, ff = gate_local.shape
    rows = weight.shape[0]
    weight_bf = weight.astype(jnp.bfloat16)
    per = tok // BLOCK_TOK

    gate_f, up_f, sigma_gate, active, hidden = swish_parts(gate_local, up_local)
    hid_send = hidden.reshape(tok, n, rows).transpose(1, 0, 2)

    def dhid_of(blk):
        return lax.dot_general(
            blk, weight_bf, (((1,), (1,)), ((), ())), preferred_element_type=jnp.float32
        ).astype(jnp.bfloat16)

    def piece(dest):
        return lax.dynamic_index_in_dim(hid_send, dest, 0, keepdims=False)

    def grad_of(blk, hid):
        total = None
        for b in range(per):
            rs = slice(b * BLOCK_TOK, (b + 1) * BLOCK_TOK)
            part = lax.dot_general(
                hid[rs], blk[rs], (((0,), (0,)), ((), ())), preferred_element_type=jnp.float32
            ).astype(jnp.bfloat16).astype(jnp.float32)
            total = part if total is None else total + part
        return total

    dbuf = jnp.zeros((n, tok, rows), jnp.bfloat16)

    def put(buf, blk, idx, valid):
        return lax.dynamic_update_slice(buf, blk[None], (jnp.where(valid, idx, f), 0, 0))

    partner = [(i, i ^ 1) for i in range(n)]
    grad = grad_of(cot_local, piece(f))
    blk = lax.ppermute(cot_local, "fsdp", partner)
    hid = lax.ppermute(piece(f ^ 1), "fsdp", partner)
    dbuf = put(dbuf, lax.ppermute(dhid_of(blk), "fsdp", partner), f ^ 1, True)
    grad = grad + grad_of(blk, hid)
    right = cot_local
    left = cot_local
    for t in range(1, m):
        right = lax.ppermute(
            right, "fsdp", [(2 * q + k, 2 * (q + 1) + k) for q in range(t - 1, m - 1) for k in (0, 1)]
        )
        left = lax.ppermute(
            left, "fsdp", [(2 * q + k, 2 * (q - 1) + k) for q in range(1, m - t + 1) for k in (0, 1)]
        )
        p_right = lax.ppermute(right, "fsdp", partner)
        p_left = lax.ppermute(left, "fsdp", partner)
        ok_r = z >= t
        ok_l = z + t <= m - 1
        back_r = [(2 * q + k, 2 * (q - t) + k) for q in range(t, m) for k in (0, 1)]
        back_l = [(2 * q + k, 2 * (q + t) + k) for q in range(0, m - t) for k in (0, 1)]
        back_pr = [(2 * q + k, 2 * (q - t) + 1 - k) for q in range(t, m) for k in (0, 1)]
        back_pl = [(2 * q + k, 2 * (q + t) + 1 - k) for q in range(0, m - t) for k in (0, 1)]
        arrivals = (
            (right, back_r, 2 * (z + t) + c, ok_l, f + 2 * t),
            (left, back_l, 2 * (z - t) + c, ok_r, f - 2 * t),
            (p_right, back_pr, 2 * (z + t) + 1 - c, ok_l, f + 2 * t + 1 - 2 * c),
            (p_left, back_pl, 2 * (z - t) + 1 - c, ok_r, f - 2 * t + 1 - 2 * c),
        )
        for blk, back, got, ok_got, dest in arrivals:
            there = [(b, a) for a, b in back]
            hid = lax.ppermute(piece(dest), "fsdp", there)
            dbuf = put(dbuf, lax.ppermute(dhid_of(blk), "fsdp", back), got, ok_got)
            grad = grad + grad_of(blk, hid)
    dbuf = put(dbuf, dhid_of(cot_local), f, True)
    dhid = dbuf.transpose(1, 0, 2).reshape(tok, ff).astype(jnp.float32)
    gate_grad, up_grad = swish_grads(dhid, gate_f, up_f, sigma_gate, active)

    new_first = 0.9 * first_moment[0] + 0.1 * grad
    new_second = 0.95 * second_moment[0] + 0.05 * grad * grad
    update = new_first / 0.6513215599 / (jnp.sqrt(new_second / 0.4012630607) + 1e-08) + 0.1 * weight
    new_weight = weight - 0.001 * update
    clusters = lax.axis_size("cluster")
    total = cluster_sum(pseudo_grad[0].astype(jnp.bfloat16), clusters)
    mean_delta = total / clusters
    new_momentum = 0.9 * outer_momentum + mean_delta
    new_outer = outer_params - 0.7 * (mean_delta + 0.9 * new_momentum)
    return (
        gate_grad[None],
        up_grad[None],
        new_weight[None],
        new_first[None],
        new_second[None],
        new_outer,
        new_momentum,
    )


def solution(mesh):
    in_specs = (
        P("cluster", "fsdp", None),
        P("cluster", "fsdp", None),
        P("cluster", "fsdp", None),
        P("cluster", "fsdp", None),
        P("cluster", "fsdp", None),
        P("cluster", "fsdp", None),
        P("cluster", "fsdp", None),
        P("fsdp", None),
        P("fsdp", None),
    )
    out_specs = (
        P("cluster", "fsdp", None),
        P("cluster", "fsdp", None),
        P("cluster", "fsdp", None),
        P("cluster", "fsdp", None),
        P("cluster", "fsdp", None),
        P("fsdp", None),
        P("fsdp", None),
    )
    return jax.shard_map(shards, mesh=mesh, in_specs=in_specs, out_specs=out_specs, check_vma=False)
```

```python
import jax
import jax.numpy as jnp
from jax import lax
from jax.sharding import PartitionSpec as P

BLOCK_TOK = 256


def swish_parts(gate_pre, up_pre):
    gate_f = gate_pre.astype(jnp.float32)
    up_f = up_pre.astype(jnp.float32)
    sigma_gate = jax.nn.sigmoid(gate_f)
    active = gate_f * sigma_gate
    hidden = (active * up_f).astype(jnp.bfloat16)
    return (gate_f, up_f, sigma_gate, active, hidden)


def swish_grads(dhid, gate_f, up_f, sigma_gate, active):
    gate_grad = (dhid * up_f * sigma_gate * (1.0 + gate_f * (1.0 - sigma_gate))).astype(
        jnp.bfloat16
    )
    up_grad = (dhid * active).astype(jnp.bfloat16)
    return (gate_grad, up_grad)


def cluster_sum(delta_bf, clusters):
    held = delta_bf[None]
    if clusters & (clusters - 1) == 0:
        step = 1
        while step < clusters:
            perm = [(i, i ^ step) for i in range(clusters)]
            held = jnp.concatenate([held, lax.ppermute(held, "cluster", perm)], axis=0)
            step *= 2
    else:
        parts = [held]
        for s in range(1, clusters):
            perm = [(i, (i + s) % clusters) for i in range(clusters)]
            parts.append(lax.ppermute(held, "cluster", perm))
        held = jnp.concatenate(parts, axis=0)
    return jnp.sum(held.astype(jnp.float32), axis=0)


def shards(
    gate_pre,
    up_pre,
    cotangent,
    down_weight,
    first_moment,
    second_moment,
    pseudo_grad,
    outer_params,
    outer_momentum,
):
    n = lax.axis_size("fsdp")
    m = n // 2
    f = lax.axis_index("fsdp")
    z = f // 2
    c = f % 2
    gate_local = gate_pre[0]
    up_local = up_pre[0]
    cot_local = cotangent[0]
    weight = down_weight[0]
    tok, ff = gate_local.shape
    rows = weight.shape[0]
    weight_bf = weight.astype(jnp.bfloat16)
    per = tok // BLOCK_TOK

    gate_f, up_f, sigma_gate, active, hidden = swish_parts(gate_local, up_local)
    hid_send = hidden.reshape(tok, n, rows).transpose(1, 0, 2)
    hid_cols = lax.all_to_all(hid_send, "fsdp", 0, 0, tiled=True)
    cot_go, hid_cols = lax.optimization_barrier((cot_local, hid_cols))

    def dhid_of(blk):
        return lax.dot_general(
            blk, weight_bf, (((1,), (1,)), ((), ())), preferred_element_type=jnp.float32
        ).astype(jnp.bfloat16)

    def grad_of(blk, src):
        hid = lax.dynamic_index_in_dim(hid_cols, src, 0, keepdims=False)
        total = None
        for b in range(per):
            rs = slice(b * BLOCK_TOK, (b + 1) * BLOCK_TOK)
            part = lax.dot_general(
                hid[rs], blk[rs], (((0,), (0,)), ((), ())), preferred_element_type=jnp.float32
            ).astype(jnp.bfloat16).astype(jnp.float32)
            total = part if total is None else total + part
        return total

    dsend = jnp.zeros((n, tok, rows), jnp.bfloat16)

    def take(dsend, grad, blk, src, ok):
        idx = jnp.where(ok, src, f)
        dsend = lax.dynamic_update_slice(dsend, dhid_of(blk)[None], (idx, 0, 0))
        return dsend, grad + grad_of(blk, idx)

    partner = [(i, i ^ 1) for i in range(n)]
    grad = grad_of(cot_go, f)
    dsend, grad = take(dsend, grad, lax.ppermute(cot_go, "fsdp", partner), f ^ 1, True)
    right = cot_go
    left = cot_go
    for t in range(1, m):
        right = lax.ppermute(
            right, "fsdp", [(2 * q + k, 2 * (q + 1) + k) for q in range(t - 1, m - 1) for k in (0, 1)]
        )
        left = lax.ppermute(
            left, "fsdp", [(2 * q + k, 2 * (q - 1) + k) for q in range(1, m - t + 1) for k in (0, 1)]
        )
        ok_r = z >= t
        ok_l = z + t <= m - 1
        dsend, grad = take(dsend, grad, right, 2 * (z - t) + c, ok_r)
        dsend, grad = take(dsend, grad, left, 2 * (z + t) + c, ok_l)
        dsend, grad = take(
            dsend, grad, lax.ppermute(right, "fsdp", partner), 2 * (z - t) + 1 - c, ok_r
        )
        dsend, grad = take(
            dsend, grad, lax.ppermute(left, "fsdp", partner), 2 * (z + t) + 1 - c, ok_l
        )
    dsend = lax.dynamic_update_slice(dsend, dhid_of(cot_go)[None], (f, 0, 0))
    dhid_recv = lax.all_to_all(dsend, "fsdp", 0, 0, tiled=True)
    dhid = dhid_recv.transpose(1, 0, 2).reshape(tok, ff).astype(jnp.float32)
    gate_grad, up_grad = swish_grads(dhid, gate_f, up_f, sigma_gate, active)

    new_first = 0.9 * first_moment[0] + 0.1 * grad
    new_second = 0.95 * second_moment[0] + 0.05 * grad * grad
    update = new_first / 0.6513215599 / (jnp.sqrt(new_second / 0.4012630607) + 1e-08) + 0.1 * weight
    new_weight = weight - 0.001 * update
    clusters = lax.axis_size("cluster")
    total = cluster_sum(pseudo_grad[0].astype(jnp.bfloat16), clusters)
    mean_delta = total / clusters
    new_momentum = 0.9 * outer_momentum + mean_delta
    new_outer = outer_params - 0.7 * (mean_delta + 0.9 * new_momentum)
    return (
        gate_grad[None],
        up_grad[None],
        new_weight[None],
        new_first[None],
        new_second[None],
        new_outer,
        new_momentum,
    )


def solution(mesh):
    in_specs = (
        P("cluster", "fsdp", None),
        P("cluster", "fsdp", None),
        P("cluster", "fsdp", None),
        P("cluster", "fsdp", None),
        P("cluster", "fsdp", None),
        P("cluster", "fsdp", None),
        P("cluster", "fsdp", None),
        P("fsdp", None),
        P("fsdp", None),
    )
    out_specs = (
        P("cluster", "fsdp", None),
        P("cluster", "fsdp", None),
        P("cluster", "fsdp", None),
        P("cluster", "fsdp", None),
        P("cluster", "fsdp", None),
        P("fsdp", None),
        P("fsdp", None),
    )
    return jax.shard_map(shards, mesh=mesh, in_specs=in_specs, out_specs=out_specs, check_vma=False)
```

```python
import jax
import jax.numpy as jnp
from jax import lax
from jax.sharding import PartitionSpec as P

BLOCK_TOK = 256


def swish_parts(gate_pre, up_pre):
    gate_f = gate_pre.astype(jnp.float32)
    up_f = up_pre.astype(jnp.float32)
    sigma_gate = jax.nn.sigmoid(gate_f)
    active = gate_f * sigma_gate
    hidden = (active * up_f).astype(jnp.bfloat16)
    return (gate_f, up_f, sigma_gate, active, hidden)


def swish_grads(dhid, gate_f, up_f, sigma_gate, active):
    gate_grad = (dhid * up_f * sigma_gate * (1.0 + gate_f * (1.0 - sigma_gate))).astype(
        jnp.bfloat16
    )
    up_grad = (dhid * active).astype(jnp.bfloat16)
    return (gate_grad, up_grad)


def cluster_sum(delta_bf, clusters):
    held = delta_bf[None]
    if clusters & (clusters - 1) == 0:
        step = 1
        while step < clusters:
            perm = [(i, i ^ step) for i in range(clusters)]
            held = jnp.concatenate([held, lax.ppermute(held, "cluster", perm)], axis=0)
            step *= 2
    else:
        parts = [held]
        for s in range(1, clusters):
            perm = [(i, (i + s) % clusters) for i in range(clusters)]
            parts.append(lax.ppermute(held, "cluster", perm))
        held = jnp.concatenate(parts, axis=0)
    return jnp.sum(held.astype(jnp.float32), axis=0)


def shards(
    gate_pre,
    up_pre,
    cotangent,
    down_weight,
    first_moment,
    second_moment,
    pseudo_grad,
    outer_params,
    outer_momentum,
):
    n = lax.axis_size("fsdp")
    m = n // 2
    f = lax.axis_index("fsdp")
    z = f // 2
    c = f % 2
    gate_local = gate_pre[0]
    up_local = up_pre[0]
    cot_local = cotangent[0]
    weight = down_weight[0]
    tok, ff = gate_local.shape
    rows = weight.shape[0]
    weight_bf = weight.astype(jnp.bfloat16)
    per = tok // BLOCK_TOK

    gate_f, up_f, sigma_gate, active, hidden = swish_parts(gate_local, up_local)
    hid_send = hidden.reshape(tok, n, rows).transpose(1, 0, 2)
    hid_cols = lax.all_to_all(hid_send, "fsdp", 0, 0, tiled=True)
    cot_go = cot_local

    def dhid_of(blk):
        return lax.dot_general(
            blk, weight_bf, (((1,), (1,)), ((), ())), preferred_element_type=jnp.float32
        ).astype(jnp.bfloat16)

    def grad_of(blk, src):
        hid = lax.dynamic_index_in_dim(hid_cols, src, 0, keepdims=False)
        total = None
        for b in range(per):
            rs = slice(b * BLOCK_TOK, (b + 1) * BLOCK_TOK)
            part = lax.dot_general(
                hid[rs], blk[rs], (((0,), (0,)), ((), ())), preferred_element_type=jnp.float32
            ).astype(jnp.bfloat16).astype(jnp.float32)
            total = part if total is None else total + part
        return total

    dsend = jnp.zeros((n, tok, rows), jnp.bfloat16)

    def take(dsend, grad, blk, src, ok):
        idx = jnp.where(ok, src, f)
        dsend = lax.dynamic_update_slice(dsend, dhid_of(blk)[None], (idx, 0, 0))
        return dsend, grad + grad_of(blk, idx)

    partner = [(i, i ^ 1) for i in range(n)]
    grad = grad_of(cot_go, f)
    dsend, grad = take(dsend, grad, lax.ppermute(cot_go, "fsdp", partner), f ^ 1, True)
    right = cot_go
    left = cot_go
    for t in range(1, m):
        right = lax.ppermute(
            right, "fsdp", [(2 * q + k, 2 * (q + 1) + k) for q in range(t - 1, m - 1) for k in (0, 1)]
        )
        left = lax.ppermute(
            left, "fsdp", [(2 * q + k, 2 * (q - 1) + k) for q in range(1, m - t + 1) for k in (0, 1)]
        )
        ok_r = z >= t
        ok_l = z + t <= m - 1
        dsend, grad = take(dsend, grad, right, 2 * (z - t) + c, ok_r)
        dsend, grad = take(dsend, grad, left, 2 * (z + t) + c, ok_l)
        dsend, grad = take(
            dsend, grad, lax.ppermute(right, "fsdp", partner), 2 * (z - t) + 1 - c, ok_r
        )
        dsend, grad = take(
            dsend, grad, lax.ppermute(left, "fsdp", partner), 2 * (z + t) + 1 - c, ok_l
        )
    dsend = lax.dynamic_update_slice(dsend, dhid_of(cot_go)[None], (f, 0, 0))
    dhid_recv = lax.all_to_all(dsend, "fsdp", 0, 0, tiled=True)
    dhid = dhid_recv.transpose(1, 0, 2).reshape(tok, ff).astype(jnp.float32)
    gate_grad, up_grad = swish_grads(dhid, gate_f, up_f, sigma_gate, active)

    new_first = 0.9 * first_moment[0] + 0.1 * grad
    new_second = 0.95 * second_moment[0] + 0.05 * grad * grad
    update = new_first / 0.6513215599 / (jnp.sqrt(new_second / 0.4012630607) + 1e-08) + 0.1 * weight
    new_weight = weight - 0.001 * update
    clusters = lax.axis_size("cluster")
    total = cluster_sum(pseudo_grad[0].astype(jnp.bfloat16), clusters)
    mean_delta = total / clusters
    new_momentum = 0.9 * outer_momentum + mean_delta
    new_outer = outer_params - 0.7 * (mean_delta + 0.9 * new_momentum)
    return (
        gate_grad[None],
        up_grad[None],
        new_weight[None],
        new_first[None],
        new_second[None],
        new_outer,
        new_momentum,
    )


def solution(mesh):
    in_specs = (
        P("cluster", "fsdp", None),
        P("cluster", "fsdp", None),
        P("cluster", "fsdp", None),
        P("cluster", "fsdp", None),
        P("cluster", "fsdp", None),
        P("cluster", "fsdp", None),
        P("cluster", "fsdp", None),
        P("fsdp", None),
        P("fsdp", None),
    )
    out_specs = (
        P("cluster", "fsdp", None),
        P("cluster", "fsdp", None),
        P("cluster", "fsdp", None),
        P("cluster", "fsdp", None),
        P("cluster", "fsdp", None),
        P("fsdp", None),
        P("fsdp", None),
    )
    return jax.shard_map(shards, mesh=mesh, in_specs=in_specs, out_specs=out_specs, check_vma=False)
```

```python
import jax
import jax.numpy as jnp
from jax import lax
from jax.sharding import PartitionSpec as P

BLOCK_TOK = 256


def swish_parts(gate_pre, up_pre):
    gate_f = gate_pre.astype(jnp.float32)
    up_f = up_pre.astype(jnp.float32)
    sigma_gate = jax.nn.sigmoid(gate_f)
    active = gate_f * sigma_gate
    hidden = (active * up_f).astype(jnp.bfloat16)
    return (gate_f, up_f, sigma_gate, active, hidden)


def swish_grads(dhid, gate_f, up_f, sigma_gate, active):
    gate_grad = (dhid * up_f * sigma_gate * (1.0 + gate_f * (1.0 - sigma_gate))).astype(
        jnp.bfloat16
    )
    up_grad = (dhid * active).astype(jnp.bfloat16)
    return (gate_grad, up_grad)


def cluster_sum(delta_bf, clusters):
    held = delta_bf[None]
    if clusters & (clusters - 1) == 0:
        step = 1
        while step < clusters:
            perm = [(i, i ^ step) for i in range(clusters)]
            held = jnp.concatenate([held, lax.ppermute(held, "cluster", perm)], axis=0)
            step *= 2
    else:
        parts = [held]
        for s in range(1, clusters):
            perm = [(i, (i + s) % clusters) for i in range(clusters)]
            parts.append(lax.ppermute(held, "cluster", perm))
        held = jnp.concatenate(parts, axis=0)
    return jnp.sum(held.astype(jnp.float32), axis=0)


def shards(
    gate_pre,
    up_pre,
    cotangent,
    down_weight,
    first_moment,
    second_moment,
    pseudo_grad,
    outer_params,
    outer_momentum,
):
    n = lax.axis_size("fsdp")
    m = n // 2
    f = lax.axis_index("fsdp")
    z = f // 2
    c = f % 2
    gate_local = gate_pre[0]
    up_local = up_pre[0]
    cot_local = cotangent[0]
    weight = down_weight[0]
    tok, ff = gate_local.shape
    rows = weight.shape[0]
    weight_bf = weight.astype(jnp.bfloat16)
    per = tok // BLOCK_TOK

    gate_f, up_f, sigma_gate, active, hidden = swish_parts(gate_local, up_local)
    hid_send = hidden.reshape(tok, n, rows).transpose(1, 0, 2)
    hid_cols = lax.all_to_all(hid_send, "fsdp", 0, 0, tiled=True)
    cot_go = cot_local

    def dhid_of(blk):
        return lax.dot_general(
            blk, weight_bf, (((1,), (1,)), ((), ())), preferred_element_type=jnp.float32
        ).astype(jnp.bfloat16)

    def grad_of(blk, src):
        hid = lax.dynamic_index_in_dim(hid_cols, src, 0, keepdims=False)
        total = None
        for b in range(per):
            rs = slice(b * BLOCK_TOK, (b + 1) * BLOCK_TOK)
            part = lax.dot_general(
                hid[rs], blk[rs], (((0,), (0,)), ((), ())), preferred_element_type=jnp.float32
            ).astype(jnp.bfloat16).astype(jnp.float32)
            total = part if total is None else total + part
        return total

    dsend = jnp.zeros((n, tok, rows), jnp.bfloat16)

    arrived = []

    def take(dsend, grad, blk, src, ok):
        idx = jnp.where(ok, src, f)
        arrived.append((blk, idx))
        return lax.dynamic_update_slice(dsend, dhid_of(blk)[None], (idx, 0, 0)), grad

    partner = [(i, i ^ 1) for i in range(n)]
    grad = None
    dsend, grad = take(dsend, grad, lax.ppermute(cot_go, "fsdp", partner), f ^ 1, True)
    right = cot_go
    left = cot_go
    for t in range(1, m):
        right = lax.ppermute(
            right, "fsdp", [(2 * q + k, 2 * (q + 1) + k) for q in range(t - 1, m - 1) for k in (0, 1)]
        )
        left = lax.ppermute(
            left, "fsdp", [(2 * q + k, 2 * (q - 1) + k) for q in range(1, m - t + 1) for k in (0, 1)]
        )
        ok_r = z >= t
        ok_l = z + t <= m - 1
        dsend, grad = take(dsend, grad, right, 2 * (z - t) + c, ok_r)
        dsend, grad = take(dsend, grad, left, 2 * (z + t) + c, ok_l)
        dsend, grad = take(
            dsend, grad, lax.ppermute(right, "fsdp", partner), 2 * (z - t) + 1 - c, ok_r
        )
        dsend, grad = take(
            dsend, grad, lax.ppermute(left, "fsdp", partner), 2 * (z + t) + 1 - c, ok_l
        )
    dsend = lax.dynamic_update_slice(dsend, dhid_of(cot_go)[None], (f, 0, 0))
    dsend, hid_cols = lax.optimization_barrier((dsend, hid_cols))
    dhid_recv = lax.all_to_all(dsend, "fsdp", 0, 0, tiled=True)
    grad = grad_of(cot_go, f)
    for blk, idx in arrived:
        grad = grad + grad_of(blk, idx)
    dhid = dhid_recv.transpose(1, 0, 2).reshape(tok, ff).astype(jnp.float32)
    gate_grad, up_grad = swish_grads(dhid, gate_f, up_f, sigma_gate, active)

    new_first = 0.9 * first_moment[0] + 0.1 * grad
    new_second = 0.95 * second_moment[0] + 0.05 * grad * grad
    update = new_first / 0.6513215599 / (jnp.sqrt(new_second / 0.4012630607) + 1e-08) + 0.1 * weight
    new_weight = weight - 0.001 * update
    clusters = lax.axis_size("cluster")
    total = cluster_sum(pseudo_grad[0].astype(jnp.bfloat16), clusters)
    mean_delta = total / clusters
    new_momentum = 0.9 * outer_momentum + mean_delta
    new_outer = outer_params - 0.7 * (mean_delta + 0.9 * new_momentum)
    return (
        gate_grad[None],
        up_grad[None],
        new_weight[None],
        new_first[None],
        new_second[None],
        new_outer,
        new_momentum,
    )


def solution(mesh):
    in_specs = (
        P("cluster", "fsdp", None),
        P("cluster", "fsdp", None),
        P("cluster", "fsdp", None),
        P("cluster", "fsdp", None),
        P("cluster", "fsdp", None),
        P("cluster", "fsdp", None),
        P("cluster", "fsdp", None),
        P("fsdp", None),
        P("fsdp", None),
    )
    out_specs = (
        P("cluster", "fsdp", None),
        P("cluster", "fsdp", None),
        P("cluster", "fsdp", None),
        P("cluster", "fsdp", None),
        P("cluster", "fsdp", None),
        P("fsdp", None),
        P("fsdp", None),
    )
    return jax.shard_map(shards, mesh=mesh, in_specs=in_specs, out_specs=out_specs, check_vma=False)
```

```python
import jax
import jax.numpy as jnp
from jax import lax
from jax.sharding import PartitionSpec as P

BLOCK_TOK = 256


def swish_parts(gate_pre, up_pre):
    gate_f = gate_pre.astype(jnp.float32)
    up_f = up_pre.astype(jnp.float32)
    sigma_gate = jax.nn.sigmoid(gate_f)
    active = gate_f * sigma_gate
    hidden = (active * up_f).astype(jnp.bfloat16)
    return (gate_f, up_f, sigma_gate, active, hidden)


def swish_grads(dhid, gate_f, up_f, sigma_gate, active):
    gate_grad = (dhid * up_f * sigma_gate * (1.0 + gate_f * (1.0 - sigma_gate))).astype(
        jnp.bfloat16
    )
    up_grad = (dhid * active).astype(jnp.bfloat16)
    return (gate_grad, up_grad)


def cluster_sum(delta_bf, clusters):
    held = delta_bf[None]
    if clusters & (clusters - 1) == 0:
        step = 1
        while step < clusters:
            perm = [(i, i ^ step) for i in range(clusters)]
            held = jnp.concatenate([held, lax.ppermute(held, "cluster", perm)], axis=0)
            step *= 2
    else:
        parts = [held]
        for s in range(1, clusters):
            perm = [(i, (i + s) % clusters) for i in range(clusters)]
            parts.append(lax.ppermute(held, "cluster", perm))
        held = jnp.concatenate(parts, axis=0)
    return jnp.sum(held.astype(jnp.float32), axis=0)


def shards(
    gate_pre,
    up_pre,
    cotangent,
    down_weight,
    first_moment,
    second_moment,
    pseudo_grad,
    outer_params,
    outer_momentum,
):
    n = lax.axis_size("fsdp")
    m = n // 2
    f = lax.axis_index("fsdp")
    z = f // 2
    c = f % 2
    gate_local = gate_pre[0]
    up_local = up_pre[0]
    cot_local = cotangent[0]
    weight = down_weight[0]
    tok, ff = gate_local.shape
    rows = weight.shape[0]
    weight_bf = weight.astype(jnp.bfloat16)
    per = tok // BLOCK_TOK

    gate_f, up_f, sigma_gate, active, hidden = swish_parts(gate_local, up_local)
    hid_send = hidden.reshape(tok, n, rows).transpose(1, 0, 2)
    hid_cols = lax.all_to_all(hid_send, "fsdp", 0, 0, tiled=True)
    cot_go = cot_local

    def dhid_of(blk):
        return lax.dot_general(
            blk, weight_bf, (((1,), (1,)), ((), ())), preferred_element_type=jnp.float32
        ).astype(jnp.bfloat16)

    def grad_of(blk, src):
        hid = lax.dynamic_index_in_dim(hid_cols, src, 0, keepdims=False)
        total = None
        for b in range(per):
            rs = slice(b * BLOCK_TOK, (b + 1) * BLOCK_TOK)
            part = lax.dot_general(
                hid[rs], blk[rs], (((0,), (0,)), ((), ())), preferred_element_type=jnp.float32
            ).astype(jnp.bfloat16).astype(jnp.float32)
            total = part if total is None else total + part
        return total

    partner = [(i, i ^ 1) for i in range(n)]

    def gather_pass(x):
        dsend = jnp.zeros((n,) + x.shape[:1] + (rows,), jnp.bfloat16)
        arrived = []

        def take(dsend, blk, src, ok):
            idx = jnp.where(ok, src, f)
            arrived.append((blk, idx))
            return lax.dynamic_update_slice(dsend, dhid_of(blk)[None], (idx, 0, 0))

        dsend = take(dsend, lax.ppermute(x, "fsdp", partner), f ^ 1, True)
        right = x
        left = x
        for t in range(1, m):
            right = lax.ppermute(
                right, "fsdp",
                [(2 * q + k, 2 * (q + 1) + k) for q in range(t - 1, m - 1) for k in (0, 1)],
            )
            left = lax.ppermute(
                left, "fsdp",
                [(2 * q + k, 2 * (q - 1) + k) for q in range(1, m - t + 1) for k in (0, 1)],
            )
            ok_r = z >= t
            ok_l = z + t <= m - 1
            dsend = take(dsend, right, 2 * (z - t) + c, ok_r)
            dsend = take(dsend, left, 2 * (z + t) + c, ok_l)
            dsend = take(dsend, lax.ppermute(right, "fsdp", partner), 2 * (z - t) + 1 - c, ok_r)
            dsend = take(dsend, lax.ppermute(left, "fsdp", partner), 2 * (z + t) + 1 - c, ok_l)
        dsend = lax.dynamic_update_slice(dsend, dhid_of(x)[None], (f, 0, 0))
        return dsend, arrived

    half = tok // 2
    dsend_a, arrived_a = gather_pass(cot_go[:half])
    recv_a = lax.all_to_all(dsend_a, "fsdp", 0, 0, tiled=True)
    dsend_b, arrived_b = gather_pass(cot_go[half:])
    dsend_b, hid_cols = lax.optimization_barrier((dsend_b, hid_cols))
    recv_b = lax.all_to_all(dsend_b, "fsdp", 0, 0, tiled=True)
    grad = grad_of(cot_go, f)
    for (blk_a, idx), (blk_b, _) in zip(arrived_a, arrived_b):
        grad = grad + grad_of(jnp.concatenate([blk_a, blk_b], axis=0), idx)
    dhid_recv = jnp.concatenate([recv_a, recv_b], axis=1)
    dhid = dhid_recv.transpose(1, 0, 2).reshape(tok, ff).astype(jnp.float32)
    gate_grad, up_grad = swish_grads(dhid, gate_f, up_f, sigma_gate, active)

    new_first = 0.9 * first_moment[0] + 0.1 * grad
    new_second = 0.95 * second_moment[0] + 0.05 * grad * grad
    update = new_first / 0.6513215599 / (jnp.sqrt(new_second / 0.4012630607) + 1e-08) + 0.1 * weight
    new_weight = weight - 0.001 * update
    clusters = lax.axis_size("cluster")
    total = cluster_sum(pseudo_grad[0].astype(jnp.bfloat16), clusters)
    mean_delta = total / clusters
    new_momentum = 0.9 * outer_momentum + mean_delta
    new_outer = outer_params - 0.7 * (mean_delta + 0.9 * new_momentum)
    return (
        gate_grad[None],
        up_grad[None],
        new_weight[None],
        new_first[None],
        new_second[None],
        new_outer,
        new_momentum,
    )


def solution(mesh):
    in_specs = (
        P("cluster", "fsdp", None),
        P("cluster", "fsdp", None),
        P("cluster", "fsdp", None),
        P("cluster", "fsdp", None),
        P("cluster", "fsdp", None),
        P("cluster", "fsdp", None),
        P("cluster", "fsdp", None),
        P("fsdp", None),
        P("fsdp", None),
    )
    out_specs = (
        P("cluster", "fsdp", None),
        P("cluster", "fsdp", None),
        P("cluster", "fsdp", None),
        P("cluster", "fsdp", None),
        P("cluster", "fsdp", None),
        P("fsdp", None),
        P("fsdp", None),
    )
    return jax.shard_map(shards, mesh=mesh, in_specs=in_specs, out_specs=out_specs, check_vma=False)
```

```python
import jax
import jax.numpy as jnp
from jax import lax
from jax.experimental.layout import Layout, with_layout_constraint
from jax.sharding import PartitionSpec as P

BLOCK_TOK = 256


def swish_parts(gate_pre, up_pre):
    gate_f = gate_pre.astype(jnp.float32)
    up_f = up_pre.astype(jnp.float32)
    sigma_gate = jax.nn.sigmoid(gate_f)
    active = gate_f * sigma_gate
    hidden = (active * up_f).astype(jnp.bfloat16)
    return (gate_f, up_f, sigma_gate, active, hidden)


def swish_grads(dhid, gate_f, up_f, sigma_gate, active):
    gate_grad = (dhid * up_f * sigma_gate * (1.0 + gate_f * (1.0 - sigma_gate))).astype(
        jnp.bfloat16
    )
    up_grad = (dhid * active).astype(jnp.bfloat16)
    return (gate_grad, up_grad)


def cluster_sum(delta_bf, clusters):
    held = delta_bf[None]
    if clusters & (clusters - 1) == 0:
        step = 1
        while step < clusters:
            perm = [(i, i ^ step) for i in range(clusters)]
            held = jnp.concatenate([held, lax.ppermute(held, "cluster", perm)], axis=0)
            step *= 2
    else:
        parts = [held]
        for s in range(1, clusters):
            perm = [(i, (i + s) % clusters) for i in range(clusters)]
            parts.append(lax.ppermute(held, "cluster", perm))
        held = jnp.concatenate(parts, axis=0)
    return jnp.sum(held.astype(jnp.float32), axis=0)


def shards(
    gate_pre,
    up_pre,
    cotangent,
    down_weight,
    first_moment,
    second_moment,
    pseudo_grad,
    outer_params,
    outer_momentum,
):
    n = lax.axis_size("fsdp")
    m = n // 2
    f = lax.axis_index("fsdp")
    z = f // 2
    c = f % 2
    row_major = Layout((0, 1))
    gate_local = with_layout_constraint(gate_pre[0], row_major)
    up_local = with_layout_constraint(up_pre[0], row_major)
    cot_local = cotangent[0]
    weight = down_weight[0]
    tok, ff = gate_local.shape
    rows = weight.shape[0]
    weight_bf = weight.astype(jnp.bfloat16)
    per = tok // BLOCK_TOK

    gate_f, up_f, sigma_gate, active, hidden = swish_parts(gate_local, up_local)
    hid_send = hidden.reshape(tok, n, rows).transpose(1, 2, 0)
    hid_cols = lax.all_to_all(hid_send, "fsdp", 0, 0, tiled=True)
    cot_go = cot_local

    def dhid_of(blk):
        return lax.dot_general(
            blk, weight_bf, (((1,), (1,)), ((), ())), preferred_element_type=jnp.float32
        ).astype(jnp.bfloat16)

    def grad_of(blk, src):
        hid = lax.dynamic_index_in_dim(hid_cols, src, 0, keepdims=False)
        total = None
        for b in range(per):
            rs = slice(b * BLOCK_TOK, (b + 1) * BLOCK_TOK)
            part = lax.dot_general(
                hid[:, rs], blk[rs], (((1,), (0,)), ((), ())), preferred_element_type=jnp.float32
            ).astype(jnp.bfloat16).astype(jnp.float32)
            total = part if total is None else total + part
        return total

    dsend = jnp.zeros((n, tok, rows), jnp.bfloat16)

    arrived = []

    def take(dsend, grad, blk, src, ok):
        idx = jnp.where(ok, src, f)
        arrived.append((blk, idx))
        return lax.dynamic_update_slice(dsend, dhid_of(blk)[None], (idx, 0, 0)), grad

    partner = [(i, i ^ 1) for i in range(n)]
    grad = None
    dsend, grad = take(dsend, grad, lax.ppermute(cot_go, "fsdp", partner), f ^ 1, True)
    right = cot_go
    left = cot_go
    for t in range(1, m):
        right = lax.ppermute(
            right, "fsdp", [(2 * q + k, 2 * (q + 1) + k) for q in range(t - 1, m - 1) for k in (0, 1)]
        )
        left = lax.ppermute(
            left, "fsdp", [(2 * q + k, 2 * (q - 1) + k) for q in range(1, m - t + 1) for k in (0, 1)]
        )
        ok_r = z >= t
        ok_l = z + t <= m - 1
        dsend, grad = take(dsend, grad, right, 2 * (z - t) + c, ok_r)
        dsend, grad = take(dsend, grad, left, 2 * (z + t) + c, ok_l)
        dsend, grad = take(
            dsend, grad, lax.ppermute(right, "fsdp", partner), 2 * (z - t) + 1 - c, ok_r
        )
        dsend, grad = take(
            dsend, grad, lax.ppermute(left, "fsdp", partner), 2 * (z + t) + 1 - c, ok_l
        )
    dsend = lax.dynamic_update_slice(dsend, dhid_of(cot_go)[None], (f, 0, 0))
    dsend, hid_cols = lax.optimization_barrier((dsend, hid_cols))
    dhid_recv = lax.all_to_all(dsend, "fsdp", 0, 0, tiled=True)
    grad = grad_of(cot_go, f)
    for blk, idx in arrived:
        grad = grad + grad_of(blk, idx)
    dhid = dhid_recv.transpose(1, 0, 2).reshape(tok, ff).astype(jnp.float32)
    gate_grad, up_grad = swish_grads(dhid, gate_f, up_f, sigma_gate, active)

    new_first = 0.9 * first_moment[0] + 0.1 * grad
    new_second = 0.95 * second_moment[0] + 0.05 * grad * grad
    update = new_first / 0.6513215599 / (jnp.sqrt(new_second / 0.4012630607) + 1e-08) + 0.1 * weight
    new_weight = weight - 0.001 * update
    clusters = lax.axis_size("cluster")
    total = cluster_sum(pseudo_grad[0].astype(jnp.bfloat16), clusters)
    mean_delta = total / clusters
    new_momentum = 0.9 * outer_momentum + mean_delta
    new_outer = outer_params - 0.7 * (mean_delta + 0.9 * new_momentum)
    return (
        gate_grad[None],
        up_grad[None],
        new_weight[None],
        new_first[None],
        new_second[None],
        new_outer,
        new_momentum,
    )


def solution(mesh):
    in_specs = (
        P("cluster", "fsdp", None),
        P("cluster", "fsdp", None),
        P("cluster", "fsdp", None),
        P("cluster", "fsdp", None),
        P("cluster", "fsdp", None),
        P("cluster", "fsdp", None),
        P("cluster", "fsdp", None),
        P("fsdp", None),
        P("fsdp", None),
    )
    out_specs = (
        P("cluster", "fsdp", None),
        P("cluster", "fsdp", None),
        P("cluster", "fsdp", None),
        P("cluster", "fsdp", None),
        P("cluster", "fsdp", None),
        P("fsdp", None),
        P("fsdp", None),
    )
    return jax.shard_map(shards, mesh=mesh, in_specs=in_specs, out_specs=out_specs, check_vma=False)
```

```python
import jax
import jax.numpy as jnp
from jax import lax
from jax.experimental.layout import Layout, with_layout_constraint
from jax.sharding import PartitionSpec as P

BLOCK_TOK = 256


def swish_parts(gate_pre, up_pre):
    gate_f = gate_pre.astype(jnp.float32)
    up_f = up_pre.astype(jnp.float32)
    sigma_gate = jax.nn.sigmoid(gate_f)
    active = gate_f * sigma_gate
    hidden = (active * up_f).astype(jnp.bfloat16)
    return (gate_f, up_f, sigma_gate, active, hidden)


def swish_grads(dhid, gate_f, up_f, sigma_gate, active):
    gate_grad = (dhid * up_f * sigma_gate * (1.0 + gate_f * (1.0 - sigma_gate))).astype(
        jnp.bfloat16
    )
    up_grad = (dhid * active).astype(jnp.bfloat16)
    return (gate_grad, up_grad)


def cluster_sum(delta_bf, clusters):
    held = delta_bf[None]
    if clusters & (clusters - 1) == 0:
        step = 1
        while step < clusters:
            perm = [(i, i ^ step) for i in range(clusters)]
            held = jnp.concatenate([held, lax.ppermute(held, "cluster", perm)], axis=0)
            step *= 2
    else:
        parts = [held]
        for s in range(1, clusters):
            perm = [(i, (i + s) % clusters) for i in range(clusters)]
            parts.append(lax.ppermute(held, "cluster", perm))
        held = jnp.concatenate(parts, axis=0)
    return jnp.sum(held.astype(jnp.float32), axis=0)


def shards(
    gate_pre,
    up_pre,
    cotangent,
    down_weight,
    first_moment,
    second_moment,
    pseudo_grad,
    outer_params,
    outer_momentum,
):
    n = lax.axis_size("fsdp")
    m = n // 2
    f = lax.axis_index("fsdp")
    z = f // 2
    c = f % 2
    row_major = Layout((0, 1))
    gate_local = with_layout_constraint(gate_pre[0], row_major)
    up_local = with_layout_constraint(up_pre[0], row_major)
    cot_local = cotangent[0]
    weight = down_weight[0]
    tok, ff = gate_local.shape
    rows = weight.shape[0]
    weight_bf = weight.astype(jnp.bfloat16)
    per = tok // BLOCK_TOK

    gate_f, up_f, sigma_gate, active, hidden = swish_parts(gate_local, up_local)
    hid_send = hidden.reshape(tok, n, rows).transpose(1, 2, 0)
    hid_cols = lax.all_to_all(hid_send, "fsdp", 0, 0, tiled=True)
    cot_go = cot_local

    def dhid_of(blk):
        return lax.dot_general(
            blk, weight_bf, (((1,), (1,)), ((), ())), preferred_element_type=jnp.float32
        ).astype(jnp.bfloat16)

    def grad_of(blk, src):
        hid = lax.dynamic_index_in_dim(hid_cols, src, 0, keepdims=False)
        total = None
        for b in range(per):
            rs = slice(b * BLOCK_TOK, (b + 1) * BLOCK_TOK)
            part = lax.dot_general(
                hid[:, rs], blk[rs], (((1,), (0,)), ((), ())), preferred_element_type=jnp.float32
            ).astype(jnp.bfloat16).astype(jnp.float32)
            total = part if total is None else total + part
        return total

    dsend = jnp.zeros((n, tok, rows), jnp.bfloat16)

    arrived = []

    def take(dsend, grad, blk, src, ok):
        idx = jnp.where(ok, src, f)
        arrived.append((blk, idx))
        return lax.dynamic_update_slice(dsend, dhid_of(blk)[None], (idx, 0, 0)), grad

    partner = [(i, i ^ 1) for i in range(n)]
    grad = None
    dsend, grad = take(dsend, grad, lax.ppermute(cot_go, "fsdp", partner), f ^ 1, True)
    right = cot_go
    left = cot_go
    for t in range(1, m):
        right = lax.ppermute(
            right, "fsdp", [(2 * q + k, 2 * (q + 1) + k) for q in range(t - 1, m - 1) for k in (0, 1)]
        )
        left = lax.ppermute(
            left, "fsdp", [(2 * q + k, 2 * (q - 1) + k) for q in range(1, m - t + 1) for k in (0, 1)]
        )
        ok_r = z >= t
        ok_l = z + t <= m - 1
        dsend, grad = take(dsend, grad, right, 2 * (z - t) + c, ok_r)
        dsend, grad = take(dsend, grad, left, 2 * (z + t) + c, ok_l)
        dsend, grad = take(
            dsend, grad, lax.ppermute(right, "fsdp", partner), 2 * (z - t) + 1 - c, ok_r
        )
        dsend, grad = take(
            dsend, grad, lax.ppermute(left, "fsdp", partner), 2 * (z + t) + 1 - c, ok_l
        )
    dsend = lax.dynamic_update_slice(dsend, dhid_of(cot_go)[None], (f, 0, 0))
    dsend, hid_cols = lax.optimization_barrier((dsend, hid_cols))
    dhid_recv = lax.all_to_all(dsend, "fsdp", 0, 0, tiled=True)
    grad = grad_of(cot_go, f)
    for blk, idx in arrived:
        grad = grad + grad_of(blk, idx)
    dhid = with_layout_constraint(dhid_recv.transpose(1, 0, 2).reshape(tok, ff), row_major)
    gate_grad, up_grad = swish_grads(dhid, gate_f, up_f, sigma_gate, active)

    new_first = 0.9 * first_moment[0] + 0.1 * grad
    new_second = 0.95 * second_moment[0] + 0.05 * grad * grad
    update = new_first / 0.6513215599 / (jnp.sqrt(new_second / 0.4012630607) + 1e-08) + 0.1 * weight
    new_weight = weight - 0.001 * update
    clusters = lax.axis_size("cluster")
    total = cluster_sum(pseudo_grad[0].astype(jnp.bfloat16), clusters)
    mean_delta = total / clusters
    new_momentum = 0.9 * outer_momentum + mean_delta
    new_outer = outer_params - 0.7 * (mean_delta + 0.9 * new_momentum)
    return (
        gate_grad[None],
        up_grad[None],
        new_weight[None],
        new_first[None],
        new_second[None],
        new_outer,
        new_momentum,
    )


def solution(mesh):
    in_specs = (
        P("cluster", "fsdp", None),
        P("cluster", "fsdp", None),
        P("cluster", "fsdp", None),
        P("cluster", "fsdp", None),
        P("cluster", "fsdp", None),
        P("cluster", "fsdp", None),
        P("cluster", "fsdp", None),
        P("fsdp", None),
        P("fsdp", None),
    )
    out_specs = (
        P("cluster", "fsdp", None),
        P("cluster", "fsdp", None),
        P("cluster", "fsdp", None),
        P("cluster", "fsdp", None),
        P("cluster", "fsdp", None),
        P("fsdp", None),
        P("fsdp", None),
    )
    return jax.shard_map(shards, mesh=mesh, in_specs=in_specs, out_specs=out_specs, check_vma=False)
```

```python
import jax
import jax.numpy as jnp
from jax import lax
from jax.experimental.layout import Layout, with_layout_constraint
from jax.sharding import PartitionSpec as P

BLOCK_TOK = 256


def swish_parts(gate_pre, up_pre):
    gate_f = gate_pre.astype(jnp.float32)
    up_f = up_pre.astype(jnp.float32)
    sigma_gate = jax.nn.sigmoid(gate_f)
    active = gate_f * sigma_gate
    hidden = (active * up_f).astype(jnp.bfloat16)
    return (gate_f, up_f, sigma_gate, active, hidden)


def swish_grads(dhid, gate_f, up_f, sigma_gate, active):
    gate_grad = (dhid * up_f * sigma_gate * (1.0 + gate_f * (1.0 - sigma_gate))).astype(
        jnp.bfloat16
    )
    up_grad = (dhid * active).astype(jnp.bfloat16)
    return (gate_grad, up_grad)


def cluster_sum(delta_bf, clusters):
    held = delta_bf[None]
    if clusters & (clusters - 1) == 0:
        step = 1
        while step < clusters:
            perm = [(i, i ^ step) for i in range(clusters)]
            held = jnp.concatenate([held, lax.ppermute(held, "cluster", perm)], axis=0)
            step *= 2
    else:
        parts = [held]
        for s in range(1, clusters):
            perm = [(i, (i + s) % clusters) for i in range(clusters)]
            parts.append(lax.ppermute(held, "cluster", perm))
        held = jnp.concatenate(parts, axis=0)
    return jnp.sum(held.astype(jnp.float32), axis=0)


def shards(
    gate_pre,
    up_pre,
    cotangent,
    down_weight,
    first_moment,
    second_moment,
    pseudo_grad,
    outer_params,
    outer_momentum,
):
    n = lax.axis_size("fsdp")
    m = n // 2
    f = lax.axis_index("fsdp")
    z = f // 2
    c = f % 2
    row_major = Layout((0, 1))
    gate_local = with_layout_constraint(gate_pre[0], row_major)
    up_local = with_layout_constraint(up_pre[0], row_major)
    cot_local = cotangent[0]
    weight = down_weight[0]
    tok, ff = gate_local.shape
    rows = weight.shape[0]
    weight_bf = weight.astype(jnp.bfloat16)
    per = tok // BLOCK_TOK

    gate_f, up_f, sigma_gate, active, hidden = swish_parts(gate_local, up_local)
    hid_send = hidden.reshape(tok, n, rows).transpose(1, 2, 0)
    hid_cols = lax.all_to_all(hid_send, "fsdp", 0, 0, tiled=True)
    cot_go = cot_local

    def dhid_of(blk):
        return lax.dot_general(
            blk, weight_bf, (((1,), (1,)), ((), ())), preferred_element_type=jnp.float32
        ).astype(jnp.bfloat16)

    def grad_of(blk, src):
        hid = lax.dynamic_index_in_dim(hid_cols, src, 0, keepdims=False)
        total = None
        for b in range(per):
            rs = slice(b * BLOCK_TOK, (b + 1) * BLOCK_TOK)
            part = lax.dot_general(
                hid[:, rs], blk[rs], (((1,), (0,)), ((), ())), preferred_element_type=jnp.float32
            ).astype(jnp.bfloat16).astype(jnp.float32)
            total = part if total is None else total + part
        return total

    dsend = jnp.zeros((n, tok, rows), jnp.bfloat16)

    cot_buf = jnp.zeros((n,) + cot_local.shape, cot_local.dtype)

    def take(dsend, cot_buf, blk, src, ok):
        idx = jnp.where(ok, src, f)
        cot_buf = lax.dynamic_update_slice(cot_buf, blk[None], (idx, 0, 0))
        return lax.dynamic_update_slice(dsend, dhid_of(blk)[None], (idx, 0, 0)), cot_buf

    partner = [(i, i ^ 1) for i in range(n)]
    grad = None
    dsend, cot_buf = take(dsend, cot_buf, lax.ppermute(cot_go, "fsdp", partner), f ^ 1, True)
    right = cot_go
    left = cot_go
    for t in range(1, m):
        right = lax.ppermute(
            right, "fsdp", [(2 * q + k, 2 * (q + 1) + k) for q in range(t - 1, m - 1) for k in (0, 1)]
        )
        left = lax.ppermute(
            left, "fsdp", [(2 * q + k, 2 * (q - 1) + k) for q in range(1, m - t + 1) for k in (0, 1)]
        )
        ok_r = z >= t
        ok_l = z + t <= m - 1
        dsend, cot_buf = take(dsend, cot_buf, right, 2 * (z - t) + c, ok_r)
        dsend, cot_buf = take(dsend, cot_buf, left, 2 * (z + t) + c, ok_l)
        dsend, cot_buf = take(
            dsend, cot_buf, lax.ppermute(right, "fsdp", partner), 2 * (z - t) + 1 - c, ok_r
        )
        dsend, cot_buf = take(
            dsend, cot_buf, lax.ppermute(left, "fsdp", partner), 2 * (z + t) + 1 - c, ok_l
        )
    dsend = lax.dynamic_update_slice(dsend, dhid_of(cot_go)[None], (f, 0, 0))
    cot_buf = lax.dynamic_update_slice(cot_buf, cot_go[None], (f, 0, 0))
    dsend, hid_cols, cot_buf = lax.optimization_barrier((dsend, hid_cols, cot_buf))
    dhid_recv = lax.all_to_all(dsend, "fsdp", 0, 0, tiled=True)
    grad = None
    for k in range(n):
        term = grad_of(cot_buf[k], k)
        grad = term if grad is None else grad + term
    dhid = with_layout_constraint(dhid_recv.transpose(1, 0, 2).reshape(tok, ff), row_major)
    gate_grad, up_grad = swish_grads(dhid, gate_f, up_f, sigma_gate, active)

    new_first = 0.9 * first_moment[0] + 0.1 * grad
    new_second = 0.95 * second_moment[0] + 0.05 * grad * grad
    update = new_first / 0.6513215599 / (jnp.sqrt(new_second / 0.4012630607) + 1e-08) + 0.1 * weight
    new_weight = weight - 0.001 * update
    clusters = lax.axis_size("cluster")
    total = cluster_sum(pseudo_grad[0].astype(jnp.bfloat16), clusters)
    mean_delta = total / clusters
    new_momentum = 0.9 * outer_momentum + mean_delta
    new_outer = outer_params - 0.7 * (mean_delta + 0.9 * new_momentum)
    return (
        gate_grad[None],
        up_grad[None],
        new_weight[None],
        new_first[None],
        new_second[None],
        new_outer,
        new_momentum,
    )


def solution(mesh):
    in_specs = (
        P("cluster", "fsdp", None),
        P("cluster", "fsdp", None),
        P("cluster", "fsdp", None),
        P("cluster", "fsdp", None),
        P("cluster", "fsdp", None),
        P("cluster", "fsdp", None),
        P("cluster", "fsdp", None),
        P("fsdp", None),
        P("fsdp", None),
    )
    out_specs = (
        P("cluster", "fsdp", None),
        P("cluster", "fsdp", None),
        P("cluster", "fsdp", None),
        P("cluster", "fsdp", None),
        P("cluster", "fsdp", None),
        P("fsdp", None),
        P("fsdp", None),
    )
    return jax.shard_map(shards, mesh=mesh, in_specs=in_specs, out_specs=out_specs, check_vma=False)
```

```python
import jax
import jax.numpy as jnp
from jax import lax
from jax.experimental.layout import Layout, with_layout_constraint
from jax.sharding import PartitionSpec as P

BLOCK_TOK = 256


def swish_parts(gate_pre, up_pre):
    gate_f = gate_pre.astype(jnp.float32)
    up_f = up_pre.astype(jnp.float32)
    sigma_gate = jax.nn.sigmoid(gate_f)
    active = gate_f * sigma_gate
    hidden = (active * up_f).astype(jnp.bfloat16)
    return (gate_f, up_f, sigma_gate, active, hidden)


def swish_grads(dhid, gate_f, up_f, sigma_gate, active):
    gate_grad = (dhid * up_f * sigma_gate * (1.0 + gate_f * (1.0 - sigma_gate))).astype(
        jnp.bfloat16
    )
    up_grad = (dhid * active).astype(jnp.bfloat16)
    return (gate_grad, up_grad)


def cluster_sum(delta_bf, clusters):
    held = delta_bf[None]
    if clusters & (clusters - 1) == 0:
        step = 1
        while step < clusters:
            perm = [(i, i ^ step) for i in range(clusters)]
            held = jnp.concatenate([held, lax.ppermute(held, "cluster", perm)], axis=0)
            step *= 2
    else:
        parts = [held]
        for s in range(1, clusters):
            perm = [(i, (i + s) % clusters) for i in range(clusters)]
            parts.append(lax.ppermute(held, "cluster", perm))
        held = jnp.concatenate(parts, axis=0)
    return jnp.sum(held.astype(jnp.float32), axis=0)


def shards(
    gate_pre,
    up_pre,
    cotangent,
    down_weight,
    first_moment,
    second_moment,
    pseudo_grad,
    outer_params,
    outer_momentum,
):
    n = lax.axis_size("fsdp")
    m = n // 2
    f = lax.axis_index("fsdp")
    z = f // 2
    c = f % 2
    row_major = Layout((0, 1))
    gate_local = with_layout_constraint(gate_pre[0], row_major)
    up_local = with_layout_constraint(up_pre[0], row_major)
    cot_local = cotangent[0]
    weight = down_weight[0]
    tok, ff = gate_local.shape
    rows = weight.shape[0]
    weight_bf = weight.astype(jnp.bfloat16)
    per = tok // BLOCK_TOK

    gate_f, up_f, sigma_gate, active, hidden = swish_parts(gate_local, up_local)
    hid_send = hidden.reshape(tok, n, rows).transpose(1, 2, 0)
    hid_cols = lax.all_to_all(hid_send, "fsdp", 0, 0, tiled=True)
    cot_go = cot_local

    def dhid_of(blk):
        return lax.dot_general(
            blk, weight_bf, (((1,), (1,)), ((), ())), preferred_element_type=jnp.float32
        ).astype(jnp.bfloat16)

    def grad_of(blk, src):
        hid = lax.dynamic_index_in_dim(hid_cols, src, 0, keepdims=False)
        total = None
        for b in range(per):
            rs = slice(b * BLOCK_TOK, (b + 1) * BLOCK_TOK)
            part = lax.dot_general(
                hid[:, rs], blk[rs], (((1,), (0,)), ((), ())), preferred_element_type=jnp.float32
            ).astype(jnp.bfloat16).astype(jnp.float32)
            total = part if total is None else total + part
        return total

    dsend = jnp.zeros((n, tok, rows), jnp.bfloat16)

    arrived = []

    def take(dsend, grad, blk, src, ok):
        idx = jnp.where(ok, src, f)
        arrived.append((blk, idx, ok))
        return lax.dynamic_update_slice(dsend, dhid_of(blk)[None], (idx, 0, 0)), grad

    partner = [(i, i ^ 1) for i in range(n)]
    grad = None
    dsend, grad = take(dsend, grad, lax.ppermute(cot_go, "fsdp", partner), f ^ 1, True)
    right = cot_go
    left = cot_go
    for t in range(1, m):
        right = lax.ppermute(
            right, "fsdp", [(2 * q + k, 2 * (q + 1) + k) for q in range(t - 1, m - 1) for k in (0, 1)]
        )
        left = lax.ppermute(
            left, "fsdp", [(2 * q + k, 2 * (q - 1) + k) for q in range(1, m - t + 1) for k in (0, 1)]
        )
        ok_r = z >= t
        ok_l = z + t <= m - 1
        dsend, grad = take(dsend, grad, right, 2 * (z - t) + c, ok_r)
        dsend, grad = take(dsend, grad, left, 2 * (z + t) + c, ok_l)
        dsend, grad = take(
            dsend, grad, lax.ppermute(right, "fsdp", partner), 2 * (z - t) + 1 - c, ok_r
        )
        dsend, grad = take(
            dsend, grad, lax.ppermute(left, "fsdp", partner), 2 * (z + t) + 1 - c, ok_l
        )
    dsend = lax.dynamic_update_slice(dsend, dhid_of(cot_go)[None], (f, 0, 0))
    dsend, hid_cols = lax.optimization_barrier((dsend, hid_cols))
    dhid_recv = lax.all_to_all(dsend, "fsdp", 0, 0, tiled=True)
    grad = grad_of(cot_go, f)
    for blk, idx, ok in arrived:
        if ok is True:
            grad = grad + grad_of(blk, idx)
        else:
            grad = lax.cond(
                ok, lambda g, b=blk, i=idx: g + grad_of(b, i), lambda g: g, grad
            )
    dhid = with_layout_constraint(dhid_recv.transpose(1, 0, 2).reshape(tok, ff), row_major)
    gate_grad, up_grad = swish_grads(dhid, gate_f, up_f, sigma_gate, active)

    new_first = 0.9 * first_moment[0] + 0.1 * grad
    new_second = 0.95 * second_moment[0] + 0.05 * grad * grad
    update = new_first / 0.6513215599 / (jnp.sqrt(new_second / 0.4012630607) + 1e-08) + 0.1 * weight
    new_weight = weight - 0.001 * update
    clusters = lax.axis_size("cluster")
    total = cluster_sum(pseudo_grad[0].astype(jnp.bfloat16), clusters)
    mean_delta = total / clusters
    new_momentum = 0.9 * outer_momentum + mean_delta
    new_outer = outer_params - 0.7 * (mean_delta + 0.9 * new_momentum)
    return (
        gate_grad[None],
        up_grad[None],
        new_weight[None],
        new_first[None],
        new_second[None],
        new_outer,
        new_momentum,
    )


def solution(mesh):
    in_specs = (
        P("cluster", "fsdp", None),
        P("cluster", "fsdp", None),
        P("cluster", "fsdp", None),
        P("cluster", "fsdp", None),
        P("cluster", "fsdp", None),
        P("cluster", "fsdp", None),
        P("cluster", "fsdp", None),
        P("fsdp", None),
        P("fsdp", None),
    )
    out_specs = (
        P("cluster", "fsdp", None),
        P("cluster", "fsdp", None),
        P("cluster", "fsdp", None),
        P("cluster", "fsdp", None),
        P("cluster", "fsdp", None),
        P("fsdp", None),
        P("fsdp", None),
    )
    return jax.shard_map(shards, mesh=mesh, in_specs=in_specs, out_specs=out_specs, check_vma=False)
```

```python
import jax
import jax.numpy as jnp
from jax import lax
from jax.experimental.layout import Layout, with_layout_constraint
from jax.sharding import PartitionSpec as P

BLOCK_TOK = 256


def swish_parts(gate_pre, up_pre):
    gate_f = gate_pre.astype(jnp.float32)
    up_f = up_pre.astype(jnp.float32)
    sigma_gate = jax.nn.sigmoid(gate_f)
    active = gate_f * sigma_gate
    hidden = (active * up_f).astype(jnp.bfloat16)
    return (gate_f, up_f, sigma_gate, active, hidden)


def swish_grads(dhid, gate_f, up_f, sigma_gate, active):
    gate_grad = (dhid * up_f * sigma_gate * (1.0 + gate_f * (1.0 - sigma_gate))).astype(
        jnp.bfloat16
    )
    up_grad = (dhid * active).astype(jnp.bfloat16)
    return (gate_grad, up_grad)


def cluster_sum(delta_bf, clusters):
    held = delta_bf[None]
    if clusters & (clusters - 1) == 0:
        step = 1
        while step < clusters:
            perm = [(i, i ^ step) for i in range(clusters)]
            held = jnp.concatenate([held, lax.ppermute(held, "cluster", perm)], axis=0)
            step *= 2
    else:
        parts = [held]
        for s in range(1, clusters):
            perm = [(i, (i + s) % clusters) for i in range(clusters)]
            parts.append(lax.ppermute(held, "cluster", perm))
        held = jnp.concatenate(parts, axis=0)
    return jnp.sum(held.astype(jnp.float32), axis=0)


def shards(
    gate_pre,
    up_pre,
    cotangent,
    down_weight,
    first_moment,
    second_moment,
    pseudo_grad,
    outer_params,
    outer_momentum,
):
    n = lax.axis_size("fsdp")
    m = n // 2
    f = lax.axis_index("fsdp")
    z = f // 2
    c = f % 2
    row_major = Layout((0, 1))
    gate_local = with_layout_constraint(gate_pre[0], row_major)
    up_local = with_layout_constraint(up_pre[0], row_major)
    cot_local = cotangent[0]
    weight = down_weight[0]
    tok, ff = gate_local.shape
    rows = weight.shape[0]
    weight_bf = weight.astype(jnp.bfloat16)
    per = tok // BLOCK_TOK

    gate_f, up_f, sigma_gate, active, hidden = swish_parts(gate_local, up_local)
    hid_send = hidden.reshape(tok, n, rows).transpose(1, 2, 0)
    hid_cols = lax.all_to_all(hid_send, "fsdp", 0, 0, tiled=True)
    cot_go = cot_local

    def dhid_of(blk):
        return lax.dot_general(
            blk, weight_bf, (((1,), (1,)), ((), ())), preferred_element_type=jnp.float32
        ).astype(jnp.bfloat16)

    def parts_of(blk, src):
        hid = lax.dynamic_index_in_dim(hid_cols, src, 0, keepdims=False)
        return [
            lax.dot_general(
                hid[:, rs], blk[rs], (((1,), (0,)), ((), ())), preferred_element_type=jnp.float32
            ).astype(jnp.bfloat16)
            for rs in (slice(b * BLOCK_TOK, (b + 1) * BLOCK_TOK) for b in range(per))
        ]

    dsend = jnp.zeros((n, tok, rows), jnp.bfloat16)

    arrived = []

    def take(dsend, grad, blk, src, ok):
        idx = jnp.where(ok, src, f)
        arrived.append((blk, idx))
        return lax.dynamic_update_slice(dsend, dhid_of(blk)[None], (idx, 0, 0)), grad

    partner = [(i, i ^ 1) for i in range(n)]
    grad = None
    dsend, grad = take(dsend, grad, lax.ppermute(cot_go, "fsdp", partner), f ^ 1, True)
    right = cot_go
    left = cot_go
    for t in range(1, m):
        right = lax.ppermute(
            right, "fsdp", [(2 * q + k, 2 * (q + 1) + k) for q in range(t - 1, m - 1) for k in (0, 1)]
        )
        left = lax.ppermute(
            left, "fsdp", [(2 * q + k, 2 * (q - 1) + k) for q in range(1, m - t + 1) for k in (0, 1)]
        )
        ok_r = z >= t
        ok_l = z + t <= m - 1
        dsend, grad = take(dsend, grad, right, 2 * (z - t) + c, ok_r)
        dsend, grad = take(dsend, grad, left, 2 * (z + t) + c, ok_l)
        dsend, grad = take(
            dsend, grad, lax.ppermute(right, "fsdp", partner), 2 * (z - t) + 1 - c, ok_r
        )
        dsend, grad = take(
            dsend, grad, lax.ppermute(left, "fsdp", partner), 2 * (z + t) + 1 - c, ok_l
        )
    dsend = lax.dynamic_update_slice(dsend, dhid_of(cot_go)[None], (f, 0, 0))
    dsend, hid_cols = lax.optimization_barrier((dsend, hid_cols))
    dhid_recv = lax.all_to_all(dsend, "fsdp", 0, 0, tiled=True)
    parts = parts_of(cot_go, f)
    for blk, idx in arrived:
        parts += parts_of(blk, idx)
    parts = lax.optimization_barrier(parts)
    grad = sum(p.astype(jnp.float32) for p in parts)
    dhid = with_layout_constraint(dhid_recv.transpose(1, 0, 2).reshape(tok, ff), row_major)
    gate_grad, up_grad = swish_grads(dhid, gate_f, up_f, sigma_gate, active)

    new_first = 0.9 * first_moment[0] + 0.1 * grad
    new_second = 0.95 * second_moment[0] + 0.05 * grad * grad
    update = new_first / 0.6513215599 / (jnp.sqrt(new_second / 0.4012630607) + 1e-08) + 0.1 * weight
    new_weight = weight - 0.001 * update
    clusters = lax.axis_size("cluster")
    total = cluster_sum(pseudo_grad[0].astype(jnp.bfloat16), clusters)
    mean_delta = total / clusters
    new_momentum = 0.9 * outer_momentum + mean_delta
    new_outer = outer_params - 0.7 * (mean_delta + 0.9 * new_momentum)
    return (
        gate_grad[None],
        up_grad[None],
        new_weight[None],
        new_first[None],
        new_second[None],
        new_outer,
        new_momentum,
    )


def solution(mesh):
    in_specs = (
        P("cluster", "fsdp", None),
        P("cluster", "fsdp", None),
        P("cluster", "fsdp", None),
        P("cluster", "fsdp", None),
        P("cluster", "fsdp", None),
        P("cluster", "fsdp", None),
        P("cluster", "fsdp", None),
        P("fsdp", None),
        P("fsdp", None),
    )
    out_specs = (
        P("cluster", "fsdp", None),
        P("cluster", "fsdp", None),
        P("cluster", "fsdp", None),
        P("cluster", "fsdp", None),
        P("cluster", "fsdp", None),
        P("fsdp", None),
        P("fsdp", None),
    )
    return jax.shard_map(shards, mesh=mesh, in_specs=in_specs, out_specs=out_specs, check_vma=False)
```

```python
import jax
import jax.numpy as jnp
from jax import lax
from jax.experimental.layout import Layout, with_layout_constraint
from jax.sharding import PartitionSpec as P

BLOCK_TOK = 256


def swish_parts(gate_pre, up_pre):
    gate_f = gate_pre.astype(jnp.float32)
    up_f = up_pre.astype(jnp.float32)
    sigma_gate = jax.nn.sigmoid(gate_f)
    active = gate_f * sigma_gate
    hidden = (active * up_f).astype(jnp.bfloat16)
    return (gate_f, up_f, sigma_gate, active, hidden)


def swish_grads(dhid, gate_f, up_f, sigma_gate, active):
    gate_grad = (dhid * up_f * sigma_gate * (1.0 + gate_f * (1.0 - sigma_gate))).astype(
        jnp.bfloat16
    )
    up_grad = (dhid * active).astype(jnp.bfloat16)
    return (gate_grad, up_grad)


def cluster_sum(delta_bf, clusters):
    held = delta_bf[None]
    if clusters & (clusters - 1) == 0:
        step = 1
        while step < clusters:
            perm = [(i, i ^ step) for i in range(clusters)]
            held = jnp.concatenate([held, lax.ppermute(held, "cluster", perm)], axis=0)
            step *= 2
    else:
        parts = [held]
        for s in range(1, clusters):
            perm = [(i, (i + s) % clusters) for i in range(clusters)]
            parts.append(lax.ppermute(held, "cluster", perm))
        held = jnp.concatenate(parts, axis=0)
    return jnp.sum(held.astype(jnp.float32), axis=0)


def shards(
    gate_pre,
    up_pre,
    cotangent,
    down_weight,
    first_moment,
    second_moment,
    pseudo_grad,
    outer_params,
    outer_momentum,
):
    n = lax.axis_size("fsdp")
    m = n // 2
    f = lax.axis_index("fsdp")
    z = f // 2
    c = f % 2
    row_major = Layout((0, 1))
    gate_local = with_layout_constraint(gate_pre[0], row_major)
    up_local = with_layout_constraint(up_pre[0], row_major)
    cot_local = cotangent[0]
    weight = down_weight[0]
    tok, ff = gate_local.shape
    rows = weight.shape[0]
    weight_bf = weight.astype(jnp.bfloat16)
    per = tok // BLOCK_TOK

    gate_f, up_f, sigma_gate, active, hidden = swish_parts(gate_local, up_local)
    hid_send = hidden.reshape(tok, n, rows).transpose(1, 2, 0)
    hid_cols = lax.all_to_all(hid_send, "fsdp", 0, 0, tiled=True)
    cot_go = cot_local

    def dhid_of(blk):
        return lax.dot_general(
            blk, weight_bf, (((1,), (1,)), ((), ())), preferred_element_type=jnp.float32
        ).astype(jnp.bfloat16)

    def grad_of(blk, src):
        hid = lax.dynamic_index_in_dim(hid_cols, src, 0, keepdims=False)
        total = None
        for b in range(per):
            rs = slice(b * BLOCK_TOK, (b + 1) * BLOCK_TOK)
            part = lax.dot_general(
                hid[:, rs], blk[rs], (((1,), (0,)), ((), ())), preferred_element_type=jnp.float32
            ).astype(jnp.bfloat16).astype(jnp.float32)
            total = part if total is None else total + part
        return total

    dsend = jnp.zeros((n, tok, rows), jnp.bfloat16)

    arrived = []

    def take(dsend, grad, blk, src, ok):
        idx = jnp.where(ok, src, f)
        arrived.append((blk, idx))
        return lax.dynamic_update_slice(dsend, dhid_of(blk)[None], (idx, 0, 0)), grad

    partner = [(i, i ^ 1) for i in range(n)]
    grad = None
    dsend, grad = take(dsend, grad, lax.ppermute(cot_go, "fsdp", partner), f ^ 1, True)
    right = cot_go
    left = cot_go
    for t in range(1, m):
        right = lax.ppermute(
            right, "fsdp", [(2 * q + k, 2 * (q + 1) + k) for q in range(t - 1, m - 1) for k in (0, 1)]
        )
        left = lax.ppermute(
            left, "fsdp", [(2 * q + k, 2 * (q - 1) + k) for q in range(1, m - t + 1) for k in (0, 1)]
        )
        ok_r = z >= t
        ok_l = z + t <= m - 1
        dsend, grad = take(dsend, grad, right, 2 * (z - t) + c, ok_r)
        dsend, grad = take(dsend, grad, left, 2 * (z + t) + c, ok_l)
        dsend, grad = take(
            dsend, grad, lax.ppermute(right, "fsdp", partner), 2 * (z - t) + 1 - c, ok_r
        )
        dsend, grad = take(
            dsend, grad, lax.ppermute(left, "fsdp", partner), 2 * (z + t) + 1 - c, ok_l
        )
    dsend = lax.dynamic_update_slice(dsend, dhid_of(cot_go)[None], (f, 0, 0))
    dsend, hid_cols = lax.optimization_barrier((dsend, hid_cols))
    dhid_recv = lax.all_to_all(dsend, "fsdp", 0, 0, tiled=True)
    cot_cat = jnp.concatenate([cot_go] + [blk for blk, _ in arrived], axis=0)
    hid_cat = jnp.concatenate(
        [lax.dynamic_index_in_dim(hid_cols, i, 0, keepdims=False) for i in [f] + [i for _, i in arrived]],
        axis=1,
    )
    grad = lax.dot_general(
        hid_cat, cot_cat, (((1,), (0,)), ((), ())), preferred_element_type=jnp.float32
    )
    dhid = with_layout_constraint(dhid_recv.transpose(1, 0, 2).reshape(tok, ff), row_major)
    gate_grad, up_grad = swish_grads(dhid, gate_f, up_f, sigma_gate, active)

    new_first = 0.9 * first_moment[0] + 0.1 * grad
    new_second = 0.95 * second_moment[0] + 0.05 * grad * grad
    update = new_first / 0.6513215599 / (jnp.sqrt(new_second / 0.4012630607) + 1e-08) + 0.1 * weight
    new_weight = weight - 0.001 * update
    clusters = lax.axis_size("cluster")
    total = cluster_sum(pseudo_grad[0].astype(jnp.bfloat16), clusters)
    mean_delta = total / clusters
    new_momentum = 0.9 * outer_momentum + mean_delta
    new_outer = outer_params - 0.7 * (mean_delta + 0.9 * new_momentum)
    return (
        gate_grad[None],
        up_grad[None],
        new_weight[None],
        new_first[None],
        new_second[None],
        new_outer,
        new_momentum,
    )


def solution(mesh):
    in_specs = (
        P("cluster", "fsdp", None),
        P("cluster", "fsdp", None),
        P("cluster", "fsdp", None),
        P("cluster", "fsdp", None),
        P("cluster", "fsdp", None),
        P("cluster", "fsdp", None),
        P("cluster", "fsdp", None),
        P("fsdp", None),
        P("fsdp", None),
    )
    out_specs = (
        P("cluster", "fsdp", None),
        P("cluster", "fsdp", None),
        P("cluster", "fsdp", None),
        P("cluster", "fsdp", None),
        P("cluster", "fsdp", None),
        P("fsdp", None),
        P("fsdp", None),
    )
    return jax.shard_map(shards, mesh=mesh, in_specs=in_specs, out_specs=out_specs, check_vma=False)
```

```python
import jax
import jax.numpy as jnp
from jax import lax
from jax.experimental.layout import Layout, with_layout_constraint
from jax.sharding import PartitionSpec as P

BLOCK_TOK = 256


def swish_parts(gate_pre, up_pre):
    gate_f = gate_pre.astype(jnp.float32)
    up_f = up_pre.astype(jnp.float32)
    sigma_gate = jax.nn.sigmoid(gate_f)
    active = gate_f * sigma_gate
    hidden = (active * up_f).astype(jnp.bfloat16)
    return (gate_f, up_f, sigma_gate, active, hidden)


def swish_grads(dhid, gate_f, up_f, sigma_gate, active):
    gate_grad = (dhid * up_f * sigma_gate * (1.0 + gate_f * (1.0 - sigma_gate))).astype(
        jnp.bfloat16
    )
    up_grad = (dhid * active).astype(jnp.bfloat16)
    return (gate_grad, up_grad)


def cluster_sum(delta_bf, clusters):
    held = delta_bf[None]
    if clusters & (clusters - 1) == 0:
        step = 1
        while step < clusters:
            perm = [(i, i ^ step) for i in range(clusters)]
            held = jnp.concatenate([held, lax.ppermute(held, "cluster", perm)], axis=0)
            step *= 2
    else:
        parts = [held]
        for s in range(1, clusters):
            perm = [(i, (i + s) % clusters) for i in range(clusters)]
            parts.append(lax.ppermute(held, "cluster", perm))
        held = jnp.concatenate(parts, axis=0)
    return jnp.sum(held.astype(jnp.float32), axis=0)


def shards(
    gate_pre,
    up_pre,
    cotangent,
    down_weight,
    first_moment,
    second_moment,
    pseudo_grad,
    outer_params,
    outer_momentum,
):
    n = lax.axis_size("fsdp")
    m = n // 2
    f = lax.axis_index("fsdp")
    z = f // 2
    c = f % 2
    row_major = Layout((0, 1))
    gate_local = with_layout_constraint(gate_pre[0], row_major)
    up_local = with_layout_constraint(up_pre[0], row_major)
    cot_local = cotangent[0]
    weight = down_weight[0]
    tok, ff = gate_local.shape
    rows = weight.shape[0]
    weight_bf = weight.astype(jnp.bfloat16)
    per = tok // BLOCK_TOK

    gate_f, up_f, sigma_gate, active, hidden = swish_parts(gate_local, up_local)
    hid_send = hidden.reshape(tok, n, rows).transpose(1, 2, 0)
    hid_cols = lax.all_to_all(hid_send, "fsdp", 0, 0, tiled=True)
    cot_go = cot_local

    def dhid_of(blk):
        return lax.dot_general(
            blk, weight_bf, (((1,), (1,)), ((), ())), preferred_element_type=jnp.float32
        ).astype(jnp.bfloat16)

    def grad_of(blk, src):
        hid = lax.dynamic_index_in_dim(hid_cols, src, 0, keepdims=False)
        total = None
        for b in range(per):
            rs = slice(b * BLOCK_TOK, (b + 1) * BLOCK_TOK)
            part = lax.dot_general(
                hid[:, rs], blk[rs], (((1,), (0,)), ((), ())), preferred_element_type=jnp.float32
            ).astype(jnp.bfloat16).astype(jnp.float32)
            total = part if total is None else total + part
        return total

    dsend = jnp.zeros((n, tok, rows), jnp.bfloat16)

    arrived = []

    def take(dsend, grad, blk, src, ok):
        idx = jnp.where(ok, src, f)
        arrived.append((blk, idx))
        return lax.dynamic_update_slice(dsend, dhid_of(blk)[None], (idx, 0, 0)), grad

    partner = [(i, i ^ 1) for i in range(n)]
    grad = None
    dsend, grad = take(dsend, grad, lax.ppermute(cot_go, "fsdp", partner), f ^ 1, True)
    right = cot_go
    left = cot_go
    for t in range(1, m):
        right = lax.ppermute(
            right, "fsdp", [(2 * q + k, 2 * (q + 1) + k) for q in range(t - 1, m - 1) for k in (0, 1)]
        )
        left = lax.ppermute(
            left, "fsdp", [(2 * q + k, 2 * (q - 1) + k) for q in range(1, m - t + 1) for k in (0, 1)]
        )
        ok_r = z >= t
        ok_l = z + t <= m - 1
        dsend, grad = take(dsend, grad, right, 2 * (z - t) + c, ok_r)
        dsend, grad = take(dsend, grad, left, 2 * (z + t) + c, ok_l)
        dsend, grad = take(
            dsend, grad, lax.ppermute(right, "fsdp", partner), 2 * (z - t) + 1 - c, ok_r
        )
        dsend, grad = take(
            dsend, grad, lax.ppermute(left, "fsdp", partner), 2 * (z + t) + 1 - c, ok_l
        )
    dsend = lax.dynamic_update_slice(dsend, dhid_of(cot_go)[None], (f, 0, 0))
    blocks = [blk for blk, _ in arrived]
    dsend, hid_cols, blocks = lax.optimization_barrier((dsend, hid_cols, blocks))
    dhid_recv = lax.all_to_all(dsend, "fsdp", 0, 0, tiled=True)
    cot_cat = jnp.concatenate([cot_go] + blocks, axis=0)
    hid_cat = jnp.concatenate(
        [lax.dynamic_index_in_dim(hid_cols, i, 0, keepdims=False) for i in [f] + [i for _, i in arrived]],
        axis=1,
    )
    grad = lax.dot_general(
        hid_cat, cot_cat, (((1,), (0,)), ((), ())), preferred_element_type=jnp.float32
    )
    dhid = with_layout_constraint(dhid_recv.transpose(1, 0, 2).reshape(tok, ff), row_major)
    gate_grad, up_grad = swish_grads(dhid, gate_f, up_f, sigma_gate, active)

    new_first = 0.9 * first_moment[0] + 0.1 * grad
    new_second = 0.95 * second_moment[0] + 0.05 * grad * grad
    update = new_first / 0.6513215599 / (jnp.sqrt(new_second / 0.4012630607) + 1e-08) + 0.1 * weight
    new_weight = weight - 0.001 * update
    clusters = lax.axis_size("cluster")
    total = cluster_sum(pseudo_grad[0].astype(jnp.bfloat16), clusters)
    mean_delta = total / clusters
    new_momentum = 0.9 * outer_momentum + mean_delta
    new_outer = outer_params - 0.7 * (mean_delta + 0.9 * new_momentum)
    return (
        gate_grad[None],
        up_grad[None],
        new_weight[None],
        new_first[None],
        new_second[None],
        new_outer,
        new_momentum,
    )


def solution(mesh):
    in_specs = (
        P("cluster", "fsdp", None),
        P("cluster", "fsdp", None),
        P("cluster", "fsdp", None),
        P("cluster", "fsdp", None),
        P("cluster", "fsdp", None),
        P("cluster", "fsdp", None),
        P("cluster", "fsdp", None),
        P("fsdp", None),
        P("fsdp", None),
    )
    out_specs = (
        P("cluster", "fsdp", None),
        P("cluster", "fsdp", None),
        P("cluster", "fsdp", None),
        P("cluster", "fsdp", None),
        P("cluster", "fsdp", None),
        P("fsdp", None),
        P("fsdp", None),
    )
    return jax.shard_map(shards, mesh=mesh, in_specs=in_specs, out_specs=out_specs, check_vma=False)
```

```python
import jax
import jax.numpy as jnp
from jax import lax
from jax.experimental.layout import Layout, with_layout_constraint
from jax.sharding import PartitionSpec as P

BLOCK_TOK = 256


def swish_parts(gate_pre, up_pre):
    gate_f = gate_pre.astype(jnp.float32)
    up_f = up_pre.astype(jnp.float32)
    sigma_gate = jax.nn.sigmoid(gate_f)
    active = gate_f * sigma_gate
    hidden = (active * up_f).astype(jnp.bfloat16)
    return (gate_f, up_f, sigma_gate, active, hidden)


def swish_grads(dhid, gate_f, up_f, sigma_gate, active):
    gate_grad = (dhid * up_f * sigma_gate * (1.0 + gate_f * (1.0 - sigma_gate))).astype(
        jnp.bfloat16
    )
    up_grad = (dhid * active).astype(jnp.bfloat16)
    return (gate_grad, up_grad)


def cluster_sum(delta_bf, clusters):
    held = delta_bf[None]
    if clusters & (clusters - 1) == 0:
        step = 1
        while step < clusters:
            perm = [(i, i ^ step) for i in range(clusters)]
            held = jnp.concatenate([held, lax.ppermute(held, "cluster", perm)], axis=0)
            step *= 2
    else:
        parts = [held]
        for s in range(1, clusters):
            perm = [(i, (i + s) % clusters) for i in range(clusters)]
            parts.append(lax.ppermute(held, "cluster", perm))
        held = jnp.concatenate(parts, axis=0)
    return jnp.sum(held.astype(jnp.float32), axis=0)


def shards(
    gate_pre,
    up_pre,
    cotangent,
    down_weight,
    first_moment,
    second_moment,
    pseudo_grad,
    outer_params,
    outer_momentum,
):
    n = lax.axis_size("fsdp")
    m = n // 2
    f = lax.axis_index("fsdp")
    z = f // 2
    c = f % 2
    row_major = Layout((0, 1))
    gate_local = with_layout_constraint(gate_pre[0], row_major)
    up_local = with_layout_constraint(up_pre[0], row_major)
    cot_local = cotangent[0]
    weight = down_weight[0]
    tok, ff = gate_local.shape
    rows = weight.shape[0]
    weight_bf = weight.astype(jnp.bfloat16)
    per = tok // BLOCK_TOK

    gate_f, up_f, sigma_gate, active, hidden = swish_parts(gate_local, up_local)
    hid_send = hidden.reshape(tok, n, rows).transpose(1, 2, 0)
    hid_cols = lax.all_to_all(hid_send, "fsdp", 0, 0, tiled=True)
    cot_go = cot_local

    def dhid_of(blk):
        return lax.dot_general(
            blk, weight_bf, (((1,), (1,)), ((), ())), preferred_element_type=jnp.float32
        ).astype(jnp.bfloat16)

    def grad_of(blk, src):
        hid = lax.dynamic_index_in_dim(hid_cols, src, 0, keepdims=False)
        total = None
        for b in range(per):
            rs = slice(b * BLOCK_TOK, (b + 1) * BLOCK_TOK)
            part = lax.dot_general(
                hid[:, rs], blk[rs], (((1,), (0,)), ((), ())), preferred_element_type=jnp.float32
            ).astype(jnp.bfloat16).astype(jnp.float32)
            total = part if total is None else total + part
        return total

    dsend = jnp.zeros((n, tok, rows), jnp.bfloat16)

    arrived = []

    def take(dsend, grad, blk, src, ok):
        idx = jnp.where(ok, src, f)
        arrived.append((blk, idx))
        return lax.dynamic_update_slice(dsend, dhid_of(blk)[None], (idx, 0, 0)), grad

    partner = [(i, i ^ 1) for i in range(n)]
    grad = None
    dsend, grad = take(dsend, grad, lax.ppermute(cot_go, "fsdp", partner), f ^ 1, True)
    right = cot_go
    left = cot_go
    for t in range(1, m):
        right = lax.ppermute(
            right, "fsdp", [(2 * q + k, 2 * (q + 1) + k) for q in range(t - 1, m - 1) for k in (0, 1)]
        )
        left = lax.ppermute(
            left, "fsdp", [(2 * q + k, 2 * (q - 1) + k) for q in range(1, m - t + 1) for k in (0, 1)]
        )
        ok_r = z >= t
        ok_l = z + t <= m - 1
        dsend, grad = take(dsend, grad, right, 2 * (z - t) + c, ok_r)
        dsend, grad = take(dsend, grad, left, 2 * (z + t) + c, ok_l)
        dsend, grad = take(
            dsend, grad, lax.ppermute(right, "fsdp", partner), 2 * (z - t) + 1 - c, ok_r
        )
        dsend, grad = take(
            dsend, grad, lax.ppermute(left, "fsdp", partner), 2 * (z + t) + 1 - c, ok_l
        )
    dsend = lax.dynamic_update_slice(dsend, dhid_of(cot_go)[None], (f, 0, 0))
    dsend, hid_cols = lax.optimization_barrier((dsend, hid_cols))
    dhid_recv = lax.all_to_all(dsend, "fsdp", 0, 0, tiled=True)
    pending = [(cot_go, f)] + arrived
    grad = None
    for i in range(0, len(pending), 2):
        group = pending[i:i + 2]
        blk = jnp.concatenate([b for b, _ in group], axis=0)
        hid = jnp.concatenate(
            [lax.dynamic_index_in_dim(hid_cols, j, 0, keepdims=False) for _, j in group], axis=1
        )
        term = lax.dot_general(
            hid, blk, (((1,), (0,)), ((), ())), preferred_element_type=jnp.float32
        ).astype(jnp.bfloat16).astype(jnp.float32)
        grad = term if grad is None else grad + term
    dhid = with_layout_constraint(dhid_recv.transpose(1, 0, 2).reshape(tok, ff), row_major)
    gate_grad, up_grad = swish_grads(dhid, gate_f, up_f, sigma_gate, active)

    new_first = 0.9 * first_moment[0] + 0.1 * grad
    new_second = 0.95 * second_moment[0] + 0.05 * grad * grad
    update = new_first / 0.6513215599 / (jnp.sqrt(new_second / 0.4012630607) + 1e-08) + 0.1 * weight
    new_weight = weight - 0.001 * update
    clusters = lax.axis_size("cluster")
    total = cluster_sum(pseudo_grad[0].astype(jnp.bfloat16), clusters)
    mean_delta = total / clusters
    new_momentum = 0.9 * outer_momentum + mean_delta
    new_outer = outer_params - 0.7 * (mean_delta + 0.9 * new_momentum)
    return (
        gate_grad[None],
        up_grad[None],
        new_weight[None],
        new_first[None],
        new_second[None],
        new_outer,
        new_momentum,
    )


def solution(mesh):
    in_specs = (
        P("cluster", "fsdp", None),
        P("cluster", "fsdp", None),
        P("cluster", "fsdp", None),
        P("cluster", "fsdp", None),
        P("cluster", "fsdp", None),
        P("cluster", "fsdp", None),
        P("cluster", "fsdp", None),
        P("fsdp", None),
        P("fsdp", None),
    )
    out_specs = (
        P("cluster", "fsdp", None),
        P("cluster", "fsdp", None),
        P("cluster", "fsdp", None),
        P("cluster", "fsdp", None),
        P("cluster", "fsdp", None),
        P("fsdp", None),
        P("fsdp", None),
    )
    return jax.shard_map(shards, mesh=mesh, in_specs=in_specs, out_specs=out_specs, check_vma=False)
```

```python
import jax
import jax.numpy as jnp
from jax import lax
from jax.experimental.layout import Layout, with_layout_constraint
from jax.sharding import PartitionSpec as P

BLOCK_TOK = 256


def swish_parts(gate_pre, up_pre):
    gate_f = gate_pre.astype(jnp.float32)
    up_f = up_pre.astype(jnp.float32)
    sigma_gate = jax.nn.sigmoid(gate_f)
    active = gate_f * sigma_gate
    hidden = (active * up_f).astype(jnp.bfloat16)
    return (gate_f, up_f, sigma_gate, active, hidden)


def swish_grads(dhid, gate_f, up_f, sigma_gate, active):
    gate_grad = (dhid * up_f * sigma_gate * (1.0 + gate_f * (1.0 - sigma_gate))).astype(
        jnp.bfloat16
    )
    up_grad = (dhid * active).astype(jnp.bfloat16)
    return (gate_grad, up_grad)


def cluster_sum(delta_bf, clusters):
    held = delta_bf[None]
    if clusters & (clusters - 1) == 0:
        step = 1
        while step < clusters:
            perm = [(i, i ^ step) for i in range(clusters)]
            held = jnp.concatenate([held, lax.ppermute(held, "cluster", perm)], axis=0)
            step *= 2
    else:
        parts = [held]
        for s in range(1, clusters):
            perm = [(i, (i + s) % clusters) for i in range(clusters)]
            parts.append(lax.ppermute(held, "cluster", perm))
        held = jnp.concatenate(parts, axis=0)
    return jnp.sum(held.astype(jnp.float32), axis=0)


def shards(
    gate_pre,
    up_pre,
    cotangent,
    down_weight,
    first_moment,
    second_moment,
    pseudo_grad,
    outer_params,
    outer_momentum,
):
    n = lax.axis_size("fsdp")
    m = n // 2
    f = lax.axis_index("fsdp")
    z = f // 2
    c = f % 2
    row_major = Layout((0, 1))
    gate_local = with_layout_constraint(gate_pre[0], row_major)
    up_local = with_layout_constraint(up_pre[0], row_major)
    cot_local = cotangent[0]
    weight = down_weight[0]
    tok, ff = gate_local.shape
    rows = weight.shape[0]
    weight_bf = weight.astype(jnp.bfloat16)
    per = tok // BLOCK_TOK

    gate_f, up_f, sigma_gate, active, hidden = swish_parts(gate_local, up_local)
    hid_send = hidden.reshape(tok, n, rows).transpose(1, 2, 0)
    hid_cols = lax.all_to_all(hid_send, "fsdp", 0, 0, tiled=True)
    cot_go = cot_local

    def dhid_of(blk):
        return lax.dot_general(
            blk, weight_bf, (((1,), (1,)), ((), ())), preferred_element_type=jnp.float32
        ).astype(jnp.bfloat16)

    def grad_of(blk, src):
        hid = lax.dynamic_index_in_dim(hid_cols, src, 0, keepdims=False)
        total = None
        for b in range(per):
            rs = slice(b * BLOCK_TOK, (b + 1) * BLOCK_TOK)
            part = lax.dot_general(
                hid[:, rs], blk[rs], (((1,), (0,)), ((), ())), preferred_element_type=jnp.float32
            ).astype(jnp.bfloat16).astype(jnp.float32)
            total = part if total is None else total + part
        return total

    dsend = jnp.zeros((n, tok, rows), jnp.bfloat16)

    arrived = []

    def take(dsend, grad, blk, src, ok):
        idx = jnp.where(ok, src, f)
        arrived.append((blk, idx))
        return lax.dynamic_update_slice(dsend, dhid_of(blk)[None], (idx, 0, 0)), grad

    partner = [(i, i ^ 1) for i in range(n)]
    grad = None
    dsend, grad = take(dsend, grad, lax.ppermute(cot_go, "fsdp", partner), f ^ 1, True)
    right = cot_go
    left = cot_go
    for t in range(1, m):
        right = lax.ppermute(
            right, "fsdp", [(2 * q + k, 2 * (q + 1) + k) for q in range(t - 1, m - 1) for k in (0, 1)]
        )
        left = lax.ppermute(
            left, "fsdp", [(2 * q + k, 2 * (q - 1) + k) for q in range(1, m - t + 1) for k in (0, 1)]
        )
        ok_r = z >= t
        ok_l = z + t <= m - 1
        dsend, grad = take(dsend, grad, right, 2 * (z - t) + c, ok_r)
        dsend, grad = take(dsend, grad, left, 2 * (z + t) + c, ok_l)
        dsend, grad = take(
            dsend, grad, lax.ppermute(right, "fsdp", partner), 2 * (z - t) + 1 - c, ok_r
        )
        dsend, grad = take(
            dsend, grad, lax.ppermute(left, "fsdp", partner), 2 * (z + t) + 1 - c, ok_l
        )
    dsend = lax.dynamic_update_slice(dsend, dhid_of(cot_go)[None], (f, 0, 0))
    dsend, hid_cols = lax.optimization_barrier((dsend, hid_cols))
    dhid_recv = lax.all_to_all(dsend, "fsdp", 0, 0, tiled=True)
    pending = [(cot_go, f)] + arrived
    grad = None
    for i in range(0, len(pending), 4):
        group = pending[i:i + 4]
        blk = jnp.concatenate([b for b, _ in group], axis=0)
        hid = jnp.concatenate(
            [lax.dynamic_index_in_dim(hid_cols, j, 0, keepdims=False) for _, j in group], axis=1
        )
        term = lax.dot_general(
            hid, blk, (((1,), (0,)), ((), ())), preferred_element_type=jnp.float32
        ).astype(jnp.bfloat16).astype(jnp.float32)
        grad = term if grad is None else grad + term
    dhid = with_layout_constraint(dhid_recv.transpose(1, 0, 2).reshape(tok, ff), row_major)
    gate_grad, up_grad = swish_grads(dhid, gate_f, up_f, sigma_gate, active)

    new_first = 0.9 * first_moment[0] + 0.1 * grad
    new_second = 0.95 * second_moment[0] + 0.05 * grad * grad
    update = new_first / 0.6513215599 / (jnp.sqrt(new_second / 0.4012630607) + 1e-08) + 0.1 * weight
    new_weight = weight - 0.001 * update
    clusters = lax.axis_size("cluster")
    total = cluster_sum(pseudo_grad[0].astype(jnp.bfloat16), clusters)
    mean_delta = total / clusters
    new_momentum = 0.9 * outer_momentum + mean_delta
    new_outer = outer_params - 0.7 * (mean_delta + 0.9 * new_momentum)
    return (
        gate_grad[None],
        up_grad[None],
        new_weight[None],
        new_first[None],
        new_second[None],
        new_outer,
        new_momentum,
    )


def solution(mesh):
    in_specs = (
        P("cluster", "fsdp", None),
        P("cluster", "fsdp", None),
        P("cluster", "fsdp", None),
        P("cluster", "fsdp", None),
        P("cluster", "fsdp", None),
        P("cluster", "fsdp", None),
        P("cluster", "fsdp", None),
        P("fsdp", None),
        P("fsdp", None),
    )
    out_specs = (
        P("cluster", "fsdp", None),
        P("cluster", "fsdp", None),
        P("cluster", "fsdp", None),
        P("cluster", "fsdp", None),
        P("cluster", "fsdp", None),
        P("fsdp", None),
        P("fsdp", None),
    )
    return jax.shard_map(shards, mesh=mesh, in_specs=in_specs, out_specs=out_specs, check_vma=False)
```
